128 devices in a mesh: row: 8 (over x, core), col: 16 (over y, z).
Axes of the slice: x: 4, y: 4, z: 4, core: 2. Of those that a mesh axis runs over, the one named last changes fastest.
Arguments:
- front: float32 [8, 8, 4, 16, 256, 256], P(None, 'row', None, 'col'), as said below
- tile_live: int32 [60], replicated, may hold values 0 or 1
- row_target: int32 [60], replicated, may hold values from 0 to 63, as said below
- col_target: int32 [60], replicated, may hold values from 0 to 63, as said below
Outputs:
- panel_factor: float32 [8, 8, 256, 1024], P(None, 'row')
- parent_update: float32 [8, 8, 4, 16, 256, 256], P(None, 'row', None, 'col')
The draws below stay inside these ranges and needn't reach their ends.
Inputs may be any that keep to these rules, and one draw needn't show every extreme that they name: `front`: the leading 4 * 256 rows and columns, upper triangle taken from the lower, form a symmetric positive definite matrix whose eigenvalues are 0.1 or more. `row_target`: Distinct. The update tile rows m with m + 4 congruent to r mod 8 go at most 1 to positions of any one residue mod 8, and exactly 1 for some r and residue. `col_target`: Distinct, and col_target[m] mod 16 equals (m + 4) mod 16.
All inputs are finite; a program needn't handle non-finite values.
Results may differ from the reference program's by a relative error of at most 0.000098.
Values sent between devices are 32-bit elements; how exact they have to be, the bound alone decides.
No kernel may reach another device: no remote copies, remote signals or barrier semaphores. Data moves between devices by JAX's collectives and lax.ppermute only.
A program may use at most 192 MiB of HBM per device.

```python
import jax
import jax.numpy as jnp
from jax import lax

TILE = 256
NT = 64
LEAD = 4
UPD = 60
PROW = 8
PCOL = 16
TRD = 8
TCD = 4


def draw_front(key, part):
    key_base = jax.random.fold_in(key, 0)
    key_mix = jax.random.fold_in(key, 1)
    key_diag = jax.random.fold_in(key, 3)
    order_all = NT * TILE
    lead_width = LEAD * TILE
    base_vals = jax.random.normal(key_base, (order_all, order_all), jnp.float32)
    mix_vals = jax.random.randint(key_mix, (lead_width, lead_width), -3, 4).astype(jnp.float32) * 0.25
    gram = jnp.dot(mix_vals, mix_vals.T, precision=lax.Precision.HIGHEST) * (1.0 / lead_width)
    shift_vals = jax.random.uniform(key_diag, (lead_width,), jnp.float32, 0.1, 0.2)
    lead_index = jnp.arange(lead_width)
    lead_block = gram + jnp.where(lead_index[:, None] == lead_index[None, :], shift_vals[:, None], 0.0)
    col_pos = jnp.arange(order_all)[None, :]
    matrix = jnp.where(col_pos < lead_width, base_vals * (0.5 / lead_width ** 0.5), base_vals)
    matrix = lax.dynamic_update_slice(matrix, lead_block.astype(jnp.float32), (0, 0))
    return matrix.reshape(TRD, PROW, TILE, TCD, PCOL, TILE).transpose(0, 1, 3, 4, 2, 5).astype(jnp.float32)


def draw_row_target(key, part):
    key_shift, key_slot = jax.random.split(jax.random.fold_in(key, 11))
    positions = jnp.arange(UPD, dtype=jnp.int32)
    global_tile = positions + LEAD
    source_row = global_tile % PROW
    local_row = global_tile // PROW
    group_count = TRD // PROW
    shifts = jax.random.randint(key_shift, (group_count,), 0, PROW)
    target_row = (source_row + local_row + jnp.take(shifts, local_row // PROW)) % PROW
    earlier = (target_row[:, None] == target_row[None, :]) & (positions[None, :] < positions[:, None])
    arrival = jnp.sum(earlier.astype(jnp.int32), axis=1)
    scores = jax.random.randint(key_slot, (PROW, TRD), 0, 1 << 20) * TRD + jnp.arange(TRD, dtype=jnp.int32)[None, :]
    slot_perm = jnp.argsort(scores, axis=1).astype(jnp.int32)
    slot_value = slot_perm[target_row, arrival]
    return (slot_value * PROW + target_row).astype(jnp.int32)


def draw_col_target(key, part):
    key_slot = jax.random.fold_in(key, 23)
    positions = jnp.arange(UPD, dtype=jnp.int32)
    global_tile = positions + LEAD
    source_col = global_tile % PCOL
    local_col = global_tile // PCOL
    scores = jax.random.randint(key_slot, (PCOL, TCD), 0, 1 << 20) * TCD + jnp.arange(TCD, dtype=jnp.int32)[None, :]
    ranks_new = jnp.argsort(jnp.argsort(scores, axis=1), axis=1).astype(jnp.int32)
    slot_value = ranks_new[source_col, local_col]
    return (slot_value * PCOL + source_col).astype(jnp.int32)


def set_ends(values, stream_key, least, largest):
    longest = values.shape.index(max(values.shape))
    spots = []
    for shift in (0, 1):
        where = [jax.random.randint(jax.random.fold_in(stream_key, axis), (), 0, length) for axis, length in enumerate(values.shape)]
        where[longest] = (where[longest] + shift) % values.shape[longest]
        spots.append(tuple(where))
    return values.at[spots[0]].set(least).at[spots[1]].set(largest)


def setup_inputs(seed: int = 0) -> dict:
    seeds = jax.random.split(jax.random.key(seed), 5)
    front = draw_front(jax.random.fold_in(seeds[4], 71), 0)
    tile_live = set_ends((jax.random.randint(seeds[1], (UPD,), 0, 8) < 5).astype(jnp.int32), jax.random.fold_in(seeds[1], 1), 0, 1)
    row_target = draw_row_target(jax.random.fold_in(seeds[4], 71), 0)
    col_target = draw_col_target(jax.random.fold_in(seeds[4], 71), 0)
    return {"front": front, "tile_live": tile_live, "row_target": row_target, "col_target": col_target}


PRECISE = lax.Precision.HIGHEST

def reference(front, tile_live, row_target, col_target):
    order_all = NT * TILE
    lead_width = LEAD * TILE
    matrix = front.transpose(0, 1, 4, 2, 3, 5).reshape(order_all, order_all)
    lead_block = matrix[:lead_width, :lead_width]
    cholesky_lead = jnp.linalg.cholesky(jnp.tril(lead_block) + jnp.tril(lead_block, -1).T)
    live_rows = jnp.repeat(tile_live, TILE).astype(jnp.float32)
    panel_rows = matrix[lead_width:, :lead_width] * live_rows[:, None]
    factor_rows = jax.scipy.linalg.solve_triangular(cholesky_lead, panel_rows.T, lower=True).T
    complement = matrix[lead_width:, lead_width:] - jnp.dot(factor_rows, factor_rows.T, precision=PRECISE)
    factor_out = jnp.concatenate([cholesky_lead, factor_rows], axis=0).reshape(TRD, PROW, TILE, lead_width)
    update_tiles = complement.reshape(UPD, TILE, UPD, TILE).transpose(0, 2, 1, 3)
    parent_tiles = jnp.zeros((NT, NT, TILE, TILE), jnp.float32)
    parent_tiles = parent_tiles.at[row_target[:, None], col_target[None, :]].set(update_tiles)
    parent_out = parent_tiles.reshape(TRD, PROW, TCD, PCOL, TILE, TILE)
    return (factor_out, parent_out)
```

```python
import jax
import jax.numpy as jnp
from jax import lax
from jax.sharding import PartitionSpec as P

LEAD = 4
PRECISE = lax.Precision.HIGHEST


def valid_gain(valid_flags, ndims):
    return valid_flags.astype(jnp.float32).reshape((-1,) + (1,) * (ndims - 1))


def route_rows(block_now, send_local, send_valid, recv_source, recv_valid, grid_rows):
    outgoing = jnp.take(block_now, send_local, axis=0) * valid_gain(send_valid, block_now.ndim)
    outgoing = outgoing.reshape((grid_rows, -1) + block_now.shape[1:])
    incoming = lax.all_to_all(outgoing, "row", split_axis=0, concat_axis=0, tiled=True)
    incoming = incoming.reshape((-1,) + block_now.shape[1:])
    return jnp.take(incoming, recv_source, axis=0) * valid_gain(recv_valid, block_now.ndim)


def local(front, tile_live, row_target, col_target):
    grid_rows = lax.axis_size("row")
    grid_cols = lax.axis_size("col")
    my_row = lax.axis_index("row")
    my_col = lax.axis_index("col")
    rows_dev = front.shape[0]
    cols_dev = front.shape[2]
    tile = front.shape[4]
    lead_w = LEAD * tile
    per_dest = rows_dev // grid_rows
    current = front[:, 0, :, 0]
    update_count = tile_live.shape[0]

    update_index = jnp.arange(update_count, dtype=jnp.int32)
    source_row = (update_index + LEAD) % grid_rows
    target_row = row_target % grid_rows
    target_slot = row_target // grid_rows
    earlier = (
        (source_row[:, None] == source_row[None, :])
        & (target_row[:, None] == target_row[None, :])
        & (update_index[None, :] < update_index[:, None])
    )
    arrival = jnp.sum(earlier.astype(jnp.int32), axis=1)
    send_slots = jnp.arange(grid_rows * per_dest, dtype=jnp.int32)
    send_match = (
        (source_row[None, :] == my_row)
        & (target_row[None, :] == send_slots[:, None] // per_dest)
        & (arrival[None, :] == send_slots[:, None] % per_dest)
    ).astype(jnp.int32)
    send_local = jnp.sum(send_match * ((update_index + LEAD) // grid_rows)[None, :], axis=1)
    send_valid = jnp.sum(send_match, axis=1) > 0
    out_slots = jnp.arange(rows_dev, dtype=jnp.int32)
    recv_match = (
        (target_row[None, :] == my_row) & (target_slot[None, :] == out_slots[:, None])
    ).astype(jnp.int32)
    recv_source = jnp.sum(recv_match * (source_row * per_dest + arrival)[None, :], axis=1)
    recv_valid = jnp.sum(recv_match, axis=1) > 0
    source_col = (update_index + LEAD) % grid_cols
    out_cols = jnp.arange(cols_dev, dtype=jnp.int32)
    col_match = (
        (source_col[None, :] == my_col) & ((col_target // grid_cols)[None, :] == out_cols[:, None])
    ).astype(jnp.int32)
    col_local = jnp.sum(col_match * ((update_index + LEAD) // grid_cols)[None, :], axis=1)
    col_valid = jnp.sum(col_match, axis=1) > 0
    col_gain = col_valid.astype(jnp.float32)

    lead_tile = current[0, 0]
    row_tiles = lax.all_gather(lead_tile, "col")[:LEAD]
    lead_tiles = lax.all_gather(row_tiles, "row")[:LEAD]
    lead_block = lead_tiles.transpose(0, 2, 1, 3).reshape(lead_w, lead_w)
    sym = jnp.tril(lead_block) + jnp.tril(lead_block, -1).T
    chol = jnp.linalg.cholesky(sym)

    chunks = rows_dev * 2
    half = tile // 2
    panel_col = current[:, 0].reshape(chunks, half, tile)
    gathered = lax.all_to_all(panel_col, "col", split_axis=0, concat_axis=0, tiled=True)
    panel_rows = gathered[:LEAD].transpose(1, 0, 2).reshape(half, lead_w)
    my_tile_row = (my_col // 2) * grid_rows + my_row
    live = jnp.where(
        my_tile_row >= LEAD,
        jnp.take(tile_live, jnp.clip(my_tile_row - LEAD, 0, update_count - 1)),
        1,
    ).astype(jnp.float32)
    solved = jax.scipy.linalg.solve_triangular(chol, (panel_rows * live).T, lower=True).T
    start = jnp.clip(my_tile_row * tile + (my_col % 2) * half, 0, lead_w - half)
    chol_rows = lax.dynamic_slice(chol, (start, 0), (half, lead_w))
    piece = jnp.where(my_tile_row < LEAD, chol_rows, solved)
    factor_rows = lax.all_gather(piece, "col").reshape(rows_dev, tile, lead_w)

    src_row = my_col % grid_rows
    pick = jnp.arange(cols_dev, dtype=jnp.int32) * (grid_cols // grid_rows) + my_col // grid_rows
    col_src = jnp.take(factor_rows, pick, axis=0).reshape(grid_rows, -1, lead_w)
    rel = (my_row - src_row) % grid_rows
    mine = jnp.where(rel == 0, col_src[0], 0.0)
    for shift in range(1, grid_rows):
        perm = []
        for c in range(grid_cols):
            s = c % grid_rows
            perm.append((s * grid_cols + c, ((s + shift) % grid_rows) * grid_cols + c))
        mine = mine + lax.ppermute(col_src[shift], ("row", "col"), perm)
    spread = lax.all_gather(mine, "row")
    order = (src_row + jnp.arange(grid_rows, dtype=jnp.int32)) % grid_rows
    col_factor = jnp.take(spread, order, axis=0).reshape(cols_dev, tile, lead_w)

    prod = jnp.einsum("aik,bjk->abij", factor_rows, col_factor, precision=PRECISE)
    schur = current - prod

    permuted = jnp.take(schur, col_local, axis=1) * col_gain[None, :, None, None]
    parent = route_rows(permuted, send_local, send_valid, recv_source, recv_valid, grid_rows)
    return (factor_rows[:, None], parent[:, None, :, None])


def solution(mesh):
    in_specs = (P(None, "row", None, "col", None, None), P(), P(), P())
    out_specs = (P(None, "row", None, None), P(None, "row", None, "col", None, None))
    return jax.shard_map(local, mesh=mesh, in_specs=in_specs, out_specs=out_specs, check_vma=False)
```

```python
import jax
import jax.numpy as jnp
from jax import lax
from jax.sharding import PartitionSpec as P

LEAD = 4
PRECISE = lax.Precision.HIGHEST


def valid_gain(valid_flags, ndims):
    return valid_flags.astype(jnp.float32).reshape((-1,) + (1,) * (ndims - 1))


def route_rows(block_now, send_local, send_valid, recv_source, recv_valid, grid_rows):
    outgoing = jnp.take(block_now, send_local, axis=0) * valid_gain(send_valid, block_now.ndim)
    outgoing = outgoing.reshape((grid_rows, -1) + block_now.shape[1:])
    incoming = lax.all_to_all(outgoing, "row", split_axis=0, concat_axis=0, tiled=True)
    incoming = incoming.reshape((-1,) + block_now.shape[1:])
    return jnp.take(incoming, recv_source, axis=0) * valid_gain(recv_valid, block_now.ndim)


def local(front, tile_live, row_target, col_target):
    grid_rows = lax.axis_size("row")
    grid_cols = lax.axis_size("col")
    my_row = lax.axis_index("row")
    my_col = lax.axis_index("col")
    rows_dev = front.shape[0]
    cols_dev = front.shape[2]
    tile = front.shape[4]
    lead_w = LEAD * tile
    per_dest = rows_dev // grid_rows
    current = front[:, 0, :, 0]
    update_count = tile_live.shape[0]

    update_index = jnp.arange(update_count, dtype=jnp.int32)
    source_row = (update_index + LEAD) % grid_rows
    target_row = row_target % grid_rows
    target_slot = row_target // grid_rows
    earlier = (
        (source_row[:, None] == source_row[None, :])
        & (target_row[:, None] == target_row[None, :])
        & (update_index[None, :] < update_index[:, None])
    )
    arrival = jnp.sum(earlier.astype(jnp.int32), axis=1)
    send_slots = jnp.arange(grid_rows * per_dest, dtype=jnp.int32)
    send_match = (
        (source_row[None, :] == my_row)
        & (target_row[None, :] == send_slots[:, None] // per_dest)
        & (arrival[None, :] == send_slots[:, None] % per_dest)
    ).astype(jnp.int32)
    send_local = jnp.sum(send_match * ((update_index + LEAD) // grid_rows)[None, :], axis=1)
    send_valid = jnp.sum(send_match, axis=1) > 0
    out_slots = jnp.arange(rows_dev, dtype=jnp.int32)
    recv_match = (
        (target_row[None, :] == my_row) & (target_slot[None, :] == out_slots[:, None])
    ).astype(jnp.int32)
    recv_source = jnp.sum(recv_match * (source_row * per_dest + arrival)[None, :], axis=1)
    recv_valid = jnp.sum(recv_match, axis=1) > 0
    source_col = (update_index + LEAD) % grid_cols
    out_cols = jnp.arange(cols_dev, dtype=jnp.int32)
    col_match = (
        (source_col[None, :] == my_col) & ((col_target // grid_cols)[None, :] == out_cols[:, None])
    ).astype(jnp.int32)
    col_local = jnp.sum(col_match * ((update_index + LEAD) // grid_cols)[None, :], axis=1)
    col_valid = jnp.sum(col_match, axis=1) > 0
    col_gain = col_valid.astype(jnp.float32)

    lead_tile = current[0, 0]
    row_tiles = lax.all_gather(lead_tile, "col")[:LEAD]
    lead_tiles = lax.all_gather(row_tiles, "row")[:LEAD]
    lead_block = lead_tiles.transpose(0, 2, 1, 3).reshape(lead_w, lead_w)
    sym = jnp.tril(lead_block) + jnp.tril(lead_block, -1).T

    chunks = rows_dev * 2
    half = tile // 2
    panel_col = current[:, 0].reshape(chunks, half, tile)
    gathered = lax.all_to_all(panel_col, "col", split_axis=0, concat_axis=0, tiled=True)
    panel_rows = gathered[:LEAD].transpose(1, 0, 2).reshape(half, lead_w)
    my_tile_row = (my_col // 2) * grid_rows + my_row
    live = jnp.where(
        my_tile_row >= LEAD,
        jnp.take(tile_live, jnp.clip(my_tile_row - LEAD, 0, update_count - 1)),
        1,
    ).astype(jnp.float32)
    masked = panel_rows * live
    bound = 1.0 + 10.0 * jnp.sum(masked * masked)
    aug = jnp.concatenate(
        [
            jnp.concatenate([sym, masked.T], axis=1),
            jnp.concatenate([masked, jnp.where(jnp.eye(half, dtype=jnp.bool_), bound, 0.0)], axis=1),
        ],
        axis=0,
    )
    aug_factor = jnp.linalg.cholesky(aug)
    chol = aug_factor[:lead_w, :lead_w]
    solved = aug_factor[lead_w:, :lead_w]
    start = jnp.clip(my_tile_row * tile + (my_col % 2) * half, 0, lead_w - half)
    chol_rows = lax.dynamic_slice(chol, (start, 0), (half, lead_w))
    piece = jnp.where(my_tile_row < LEAD, chol_rows, solved)
    factor_rows = lax.all_gather(piece, "col").reshape(rows_dev, tile, lead_w)

    src_row = my_col % grid_rows
    pick = jnp.arange(cols_dev, dtype=jnp.int32) * (grid_cols // grid_rows) + my_col // grid_rows
    col_src = jnp.take(factor_rows, pick, axis=0).reshape(grid_rows, -1, lead_w)
    rel = (my_row - src_row) % grid_rows
    mine = jnp.where(rel == 0, col_src[0], 0.0)
    for shift in range(1, grid_rows):
        perm = []
        for c in range(grid_cols):
            s = c % grid_rows
            perm.append((s * grid_cols + c, ((s + shift) % grid_rows) * grid_cols + c))
        mine = mine + lax.ppermute(col_src[shift], ("row", "col"), perm)
    spread = lax.all_gather(mine, "row")
    order = (src_row + jnp.arange(grid_rows, dtype=jnp.int32)) % grid_rows
    col_factor = jnp.take(spread, order, axis=0).reshape(cols_dev, tile, lead_w)

    prod = jnp.einsum("aik,bjk->abij", factor_rows, col_factor, precision=PRECISE)
    schur = current - prod

    permuted = jnp.take(schur, col_local, axis=1) * col_gain[None, :, None, None]
    parent = route_rows(permuted, send_local, send_valid, recv_source, recv_valid, grid_rows)
    return (factor_rows[:, None], parent[:, None, :, None])


def solution(mesh):
    in_specs = (P(None, "row", None, "col", None, None), P(), P(), P())
    out_specs = (P(None, "row", None, None), P(None, "row", None, "col", None, None))
    return jax.shard_map(local, mesh=mesh, in_specs=in_specs, out_specs=out_specs, check_vma=False)
```

```python
import jax
import jax.numpy as jnp
from jax import lax
from jax.sharding import PartitionSpec as P

LEAD = 4
PRECISE = lax.Precision.HIGHEST


def valid_gain(valid_flags, ndims):
    return valid_flags.astype(jnp.float32).reshape((-1,) + (1,) * (ndims - 1))


def route_rows(block_now, send_local, send_valid, recv_source, recv_valid, grid_rows):
    outgoing = jnp.take(block_now, send_local, axis=0) * valid_gain(send_valid, block_now.ndim)
    outgoing = outgoing.reshape((grid_rows, -1) + block_now.shape[1:])
    incoming = lax.all_to_all(outgoing, "row", split_axis=0, concat_axis=0, tiled=True)
    incoming = incoming.reshape((-1,) + block_now.shape[1:])
    return jnp.take(incoming, recv_source, axis=0) * valid_gain(recv_valid, block_now.ndim)


def local(front, tile_live, row_target, col_target):
    grid_rows = lax.axis_size("row")
    grid_cols = lax.axis_size("col")
    my_row = lax.axis_index("row")
    my_col = lax.axis_index("col")
    rows_dev = front.shape[0]
    cols_dev = front.shape[2]
    tile = front.shape[4]
    lead_w = LEAD * tile
    per_dest = rows_dev // grid_rows
    current = front[:, 0, :, 0]
    update_count = tile_live.shape[0]

    update_index = jnp.arange(update_count, dtype=jnp.int32)
    source_row = (update_index + LEAD) % grid_rows
    target_row = row_target % grid_rows
    target_slot = row_target // grid_rows
    earlier = (
        (source_row[:, None] == source_row[None, :])
        & (target_row[:, None] == target_row[None, :])
        & (update_index[None, :] < update_index[:, None])
    )
    arrival = jnp.sum(earlier.astype(jnp.int32), axis=1)
    send_slots = jnp.arange(grid_rows * per_dest, dtype=jnp.int32)
    send_match = (
        (source_row[None, :] == my_row)
        & (target_row[None, :] == send_slots[:, None] // per_dest)
        & (arrival[None, :] == send_slots[:, None] % per_dest)
    ).astype(jnp.int32)
    send_local = jnp.sum(send_match * ((update_index + LEAD) // grid_rows)[None, :], axis=1)
    send_valid = jnp.sum(send_match, axis=1) > 0
    out_slots = jnp.arange(rows_dev, dtype=jnp.int32)
    recv_match = (
        (target_row[None, :] == my_row) & (target_slot[None, :] == out_slots[:, None])
    ).astype(jnp.int32)
    recv_source = jnp.sum(recv_match * (source_row * per_dest + arrival)[None, :], axis=1)
    recv_valid = jnp.sum(recv_match, axis=1) > 0
    source_col = (update_index + LEAD) % grid_cols
    out_cols = jnp.arange(cols_dev, dtype=jnp.int32)
    col_match = (
        (source_col[None, :] == my_col) & ((col_target // grid_cols)[None, :] == out_cols[:, None])
    ).astype(jnp.int32)
    col_local = jnp.sum(col_match * ((update_index + LEAD) // grid_cols)[None, :], axis=1)
    col_valid = jnp.sum(col_match, axis=1) > 0
    col_gain = col_valid.astype(jnp.float32)

    lead_tile = current[0, 0]
    row_tiles = lax.all_gather(lead_tile, "col")[:LEAD]
    lead_tiles = lax.all_gather(row_tiles, "row")[:LEAD]
    lead_block = lead_tiles.transpose(0, 2, 1, 3).reshape(lead_w, lead_w)
    sym = jnp.tril(lead_block) + jnp.tril(lead_block, -1).T

    chunks = rows_dev * 2
    half = tile // 2
    panel_col = current[:, 0].reshape(chunks, half, tile)
    gathered = lax.all_to_all(panel_col, "col", split_axis=0, concat_axis=0, tiled=True)
    panel_rows = gathered[:LEAD].transpose(1, 0, 2).reshape(half, lead_w)
    my_tile_row = (my_col // 2) * grid_rows + my_row
    live = jnp.where(
        my_tile_row >= LEAD,
        jnp.take(tile_live, jnp.clip(my_tile_row - LEAD, 0, update_count - 1)),
        1,
    ).astype(jnp.float32)
    masked = panel_rows * live
    bound = 1.0 + 10.0 * jnp.sum(masked * masked)
    aug = jnp.concatenate(
        [
            jnp.concatenate([sym, masked.T], axis=1),
            jnp.concatenate([masked, jnp.where(jnp.eye(half, dtype=jnp.bool_), bound, 0.0)], axis=1),
        ],
        axis=0,
    )
    aug_factor = jnp.linalg.cholesky(aug)
    chol = aug_factor[:lead_w, :lead_w]
    solved = aug_factor[lead_w:, :lead_w]
    start = jnp.clip(my_tile_row * tile + (my_col % 2) * half, 0, lead_w - half)
    chol_rows = lax.dynamic_slice(chol, (start, 0), (half, lead_w))
    piece = jnp.where(my_tile_row < LEAD, chol_rows, solved)
    factor_rows = lax.all_gather(piece, "col").reshape(rows_dev, tile, lead_w)

    src_row = my_col % grid_rows
    mine = None
    for j in range(grid_rows):
        perm = []
        for c in range(grid_cols):
            s = c % grid_rows
            source_col = 4 * (j // 2) + 2 * (c // grid_rows) + j % 2
            perm.append((s * grid_cols + source_col, ((s + j) % grid_rows) * grid_cols + c))
        moved = lax.ppermute(piece, ("row", "col"), perm)
        mine = moved if mine is None else mine + moved
    spread = lax.all_gather(mine, "row")
    order = (src_row + jnp.arange(grid_rows, dtype=jnp.int32)) % grid_rows
    col_factor = spread[order].reshape(cols_dev, tile, lead_w)

    prod = jnp.einsum("aik,bjk->abij", factor_rows, col_factor, precision=PRECISE)
    schur = (current - prod).reshape((rows_dev * cols_dev,) + current.shape[2:])

    flat_idx = send_local[:, None] * cols_dev + col_local[None, :]
    keep = (send_valid[:, None] & col_valid[None, :])[:, :, None, None]
    outgoing = jnp.where(keep, schur[flat_idx], 0.0)
    incoming = lax.all_to_all(outgoing, "row", split_axis=0, concat_axis=0, tiled=True)
    parent = jnp.where(recv_valid[:, None, None, None], incoming[recv_source], 0.0)
    return (factor_rows[:, None], parent[:, None, :, None])


def solution(mesh):
    in_specs = (P(None, "row", None, "col", None, None), P(), P(), P())
    out_specs = (P(None, "row", None, None), P(None, "row", None, "col", None, None))
    return jax.shard_map(local, mesh=mesh, in_specs=in_specs, out_specs=out_specs, check_vma=False)
```

```python
import jax
import jax.numpy as jnp
from jax import lax
from jax.sharding import PartitionSpec as P

LEAD = 4
PRECISE = lax.Precision.HIGHEST


def valid_gain(valid_flags, ndims):
    return valid_flags.astype(jnp.float32).reshape((-1,) + (1,) * (ndims - 1))


def route_rows(block_now, send_local, send_valid, recv_source, recv_valid, grid_rows):
    outgoing = jnp.take(block_now, send_local, axis=0) * valid_gain(send_valid, block_now.ndim)
    outgoing = outgoing.reshape((grid_rows, -1) + block_now.shape[1:])
    incoming = lax.all_to_all(outgoing, "row", split_axis=0, concat_axis=0, tiled=True)
    incoming = incoming.reshape((-1,) + block_now.shape[1:])
    return jnp.take(incoming, recv_source, axis=0) * valid_gain(recv_valid, block_now.ndim)


def local(front, tile_live, row_target, col_target):
    grid_rows = lax.axis_size("row")
    grid_cols = lax.axis_size("col")
    my_row = lax.axis_index("row")
    my_col = lax.axis_index("col")
    rows_dev = front.shape[0]
    cols_dev = front.shape[2]
    tile = front.shape[4]
    lead_w = LEAD * tile
    per_dest = rows_dev // grid_rows
    current = front[:, 0, :, 0]
    update_count = tile_live.shape[0]

    update_index = jnp.arange(update_count, dtype=jnp.int32)
    source_row = (update_index + LEAD) % grid_rows
    target_row = row_target % grid_rows
    target_slot = row_target // grid_rows
    earlier = (
        (source_row[:, None] == source_row[None, :])
        & (target_row[:, None] == target_row[None, :])
        & (update_index[None, :] < update_index[:, None])
    )
    arrival = jnp.sum(earlier.astype(jnp.int32), axis=1)
    send_slots = jnp.arange(grid_rows * per_dest, dtype=jnp.int32)
    send_match = (
        (source_row[None, :] == my_row)
        & (target_row[None, :] == send_slots[:, None] // per_dest)
        & (arrival[None, :] == send_slots[:, None] % per_dest)
    ).astype(jnp.int32)
    send_local = jnp.sum(send_match * ((update_index + LEAD) // grid_rows)[None, :], axis=1)
    send_valid = jnp.sum(send_match, axis=1) > 0
    out_slots = jnp.arange(rows_dev, dtype=jnp.int32)
    recv_match = (
        (target_row[None, :] == my_row) & (target_slot[None, :] == out_slots[:, None])
    ).astype(jnp.int32)
    recv_source = jnp.sum(recv_match * (source_row * per_dest + arrival)[None, :], axis=1)
    recv_valid = jnp.sum(recv_match, axis=1) > 0
    source_col = (update_index + LEAD) % grid_cols
    out_cols = jnp.arange(cols_dev, dtype=jnp.int32)
    col_match = (
        (source_col[None, :] == my_col) & ((col_target // grid_cols)[None, :] == out_cols[:, None])
    ).astype(jnp.int32)
    col_local = jnp.sum(col_match * ((update_index + LEAD) // grid_cols)[None, :], axis=1)
    col_valid = jnp.sum(col_match, axis=1) > 0
    col_gain = col_valid.astype(jnp.float32)

    lead_tile = current[0, 0]
    row_tiles = lax.all_gather(lead_tile, "col")[:LEAD]
    lead_tiles = lax.all_gather(row_tiles, "row")[:LEAD]
    lead_block = lead_tiles.transpose(0, 2, 1, 3).reshape(lead_w, lead_w)
    chunks = rows_dev * 2
    half = tile // 2
    panel_col = current[:, 0].reshape(chunks, half, tile)
    gathered = lax.all_to_all(panel_col, "col", split_axis=0, concat_axis=0, tiled=True)
    panel_rows = gathered[:LEAD].transpose(1, 0, 2).reshape(half, lead_w)
    my_tile_row = (my_col // 2) * grid_rows + my_row
    live = jnp.where(
        my_tile_row >= LEAD,
        jnp.take(tile_live, jnp.clip(my_tile_row - LEAD, 0, update_count - 1)),
        1,
    ).astype(jnp.float32)
    masked = panel_rows * live
    bound = 1.0 + 10.0 * jnp.sum(masked * masked)
    aug = jnp.concatenate(
        [
            jnp.concatenate([lead_block, jnp.zeros((lead_w, half), jnp.float32)], axis=1),
            jnp.concatenate([masked, jnp.where(jnp.eye(half, dtype=jnp.bool_), bound, 0.0)], axis=1),
        ],
        axis=0,
    )
    aug_factor = lax.linalg.cholesky(aug, symmetrize_input=False)
    chol = aug_factor[:lead_w, :lead_w]
    solved = aug_factor[lead_w:, :lead_w]
    start = jnp.clip(my_tile_row * tile + (my_col % 2) * half, 0, lead_w - half)
    chol_rows = lax.dynamic_slice(chol, (start, 0), (half, lead_w))
    piece = jnp.where(my_tile_row < LEAD, chol_rows, solved)
    factor_rows = lax.all_gather(piece, "col").reshape(rows_dev, tile, lead_w)

    src_row = my_col % grid_rows
    mine = None
    for j in range(grid_rows):
        perm = []
        for c in range(grid_cols):
            s = c % grid_rows
            source_col = 4 * (j // 2) + 2 * (c // grid_rows) + j % 2
            perm.append((s * grid_cols + source_col, ((s + j) % grid_rows) * grid_cols + c))
        moved = lax.ppermute(piece, ("row", "col"), perm)
        mine = moved if mine is None else mine + moved
    ring = [mine]
    for step in range(1, grid_rows // 2):
        perm = [(i, (i + 2 * step) % grid_rows) for i in range(grid_rows)]
        ring.append(lax.ppermute(mine, "row", perm))
    ring = jnp.stack(ring)
    partner = lax.ppermute(ring, "row", [(i, i ^ 1) for i in range(grid_rows)])
    combined = jnp.concatenate([ring, partner], axis=0)
    chunk_ids = jnp.arange(grid_rows, dtype=jnp.int32)
    own_d = (my_row - src_row - chunk_ids) % grid_rows
    par_d = ((my_row ^ 1) - src_row - chunk_ids) % grid_rows
    pos = jnp.where(own_d % 2 == 0, own_d // 2, grid_rows // 2 + par_d // 2)
    col_factor = combined[pos].reshape(cols_dev, tile, lead_w)

    prod = jnp.einsum("aik,bjk->abij", factor_rows, col_factor, precision=PRECISE)
    schur = (current - prod).reshape((rows_dev * cols_dev,) + current.shape[2:])

    flat_idx = send_local[:, None] * cols_dev + col_local[None, :]
    keep = (send_valid[:, None] & col_valid[None, :])[:, :, None, None]
    outgoing = jnp.where(keep, schur[flat_idx], 0.0)
    incoming = lax.all_to_all(outgoing, "row", split_axis=0, concat_axis=0, tiled=True)
    parent = jnp.where(recv_valid[:, None, None, None], incoming[recv_source], 0.0)
    return (factor_rows[:, None], parent[:, None, :, None])


def solution(mesh):
    in_specs = (P(None, "row", None, "col", None, None), P(), P(), P())
    out_specs = (P(None, "row", None, None), P(None, "row", None, "col", None, None))
    return jax.shard_map(local, mesh=mesh, in_specs=in_specs, out_specs=out_specs, check_vma=False)
```

```python
import jax
import jax.numpy as jnp
from jax import lax
from jax.sharding import PartitionSpec as P

LEAD = 4
PRECISE = lax.Precision.HIGHEST


def valid_gain(valid_flags, ndims):
    return valid_flags.astype(jnp.float32).reshape((-1,) + (1,) * (ndims - 1))


def route_rows(block_now, send_local, send_valid, recv_source, recv_valid, grid_rows):
    outgoing = jnp.take(block_now, send_local, axis=0) * valid_gain(send_valid, block_now.ndim)
    outgoing = outgoing.reshape((grid_rows, -1) + block_now.shape[1:])
    incoming = lax.all_to_all(outgoing, "row", split_axis=0, concat_axis=0, tiled=True)
    incoming = incoming.reshape((-1,) + block_now.shape[1:])
    return jnp.take(incoming, recv_source, axis=0) * valid_gain(recv_valid, block_now.ndim)


def spread_from_first_four(x, axis, size):
    idx = lax.axis_index(axis)
    held = jnp.where(idx < LEAD, x, 0.0)
    for q in range(1, size // LEAD):
        held = held + lax.ppermute(x, axis, [(j, j + LEAD * q) for j in range(LEAD)])
    parts = [held]
    for k in range(1, LEAD):
        perm = [(i, LEAD * (i // LEAD) + (i % LEAD + k) % LEAD) for i in range(size)]
        parts.append(lax.ppermute(held, axis, perm))
    parts = jnp.stack(parts)
    order = (idx % LEAD - jnp.arange(LEAD, dtype=jnp.int32)) % LEAD
    return parts[order]


def local(front, tile_live, row_target, col_target):
    grid_rows = lax.axis_size("row")
    grid_cols = lax.axis_size("col")
    my_row = lax.axis_index("row")
    my_col = lax.axis_index("col")
    rows_dev = front.shape[0]
    cols_dev = front.shape[2]
    tile = front.shape[4]
    lead_w = LEAD * tile
    per_dest = rows_dev // grid_rows
    current = front[:, 0, :, 0]
    update_count = tile_live.shape[0]

    update_index = jnp.arange(update_count, dtype=jnp.int32)
    source_row = (update_index + LEAD) % grid_rows
    target_row = row_target % grid_rows
    target_slot = row_target // grid_rows
    earlier = (
        (source_row[:, None] == source_row[None, :])
        & (target_row[:, None] == target_row[None, :])
        & (update_index[None, :] < update_index[:, None])
    )
    arrival = jnp.sum(earlier.astype(jnp.int32), axis=1)
    send_slots = jnp.arange(grid_rows * per_dest, dtype=jnp.int32)
    send_match = (
        (source_row[None, :] == my_row)
        & (target_row[None, :] == send_slots[:, None] // per_dest)
        & (arrival[None, :] == send_slots[:, None] % per_dest)
    ).astype(jnp.int32)
    send_local = jnp.sum(send_match * ((update_index + LEAD) // grid_rows)[None, :], axis=1)
    send_valid = jnp.sum(send_match, axis=1) > 0
    out_slots = jnp.arange(rows_dev, dtype=jnp.int32)
    recv_match = (
        (target_row[None, :] == my_row) & (target_slot[None, :] == out_slots[:, None])
    ).astype(jnp.int32)
    recv_source = jnp.sum(recv_match * (source_row * per_dest + arrival)[None, :], axis=1)
    recv_valid = jnp.sum(recv_match, axis=1) > 0
    source_col = (update_index + LEAD) % grid_cols
    out_cols = jnp.arange(cols_dev, dtype=jnp.int32)
    col_match = (
        (source_col[None, :] == my_col) & ((col_target // grid_cols)[None, :] == out_cols[:, None])
    ).astype(jnp.int32)
    col_local = jnp.sum(col_match * ((update_index + LEAD) // grid_cols)[None, :], axis=1)
    col_valid = jnp.sum(col_match, axis=1) > 0
    col_gain = col_valid.astype(jnp.float32)

    lead_tile = current[0, 0]
    col_tiles = spread_from_first_four(lead_tile, "row", grid_rows)
    lead_tiles = spread_from_first_four(col_tiles, "col", grid_cols)
    lead_block = lead_tiles.transpose(1, 2, 0, 3).reshape(lead_w, lead_w)
    chunks = rows_dev * 2
    half = tile // 2
    panel_col = current[:, 0].reshape(chunks, half, tile)
    gathered = lax.all_to_all(panel_col, "col", split_axis=0, concat_axis=0, tiled=True)
    panel_rows = gathered[:LEAD].transpose(1, 0, 2).reshape(half, lead_w)
    my_tile_row = (my_col // 2) * grid_rows + my_row
    live = jnp.where(
        my_tile_row >= LEAD,
        jnp.take(tile_live, jnp.clip(my_tile_row - LEAD, 0, update_count - 1)),
        1,
    ).astype(jnp.float32)
    masked = panel_rows * live
    bound = 1.0 + 10.0 * jnp.sum(masked * masked)
    aug = jnp.concatenate(
        [
            jnp.concatenate([lead_block, jnp.zeros((lead_w, half), jnp.float32)], axis=1),
            jnp.concatenate([masked, jnp.where(jnp.eye(half, dtype=jnp.bool_), bound, 0.0)], axis=1),
        ],
        axis=0,
    )
    aug_factor = lax.linalg.cholesky(aug, symmetrize_input=False)
    chol = aug_factor[:lead_w, :lead_w]
    solved = aug_factor[lead_w:, :lead_w]
    start = jnp.clip(my_tile_row * tile + (my_col % 2) * half, 0, lead_w - half)
    chol_rows = lax.dynamic_slice(chol, (start, 0), (half, lead_w))
    piece = jnp.where(my_tile_row < LEAD, chol_rows, solved)
    factor_rows = lax.all_gather(piece, "col").reshape(rows_dev, tile, lead_w)

    src_row = my_col % grid_rows
    mine = None
    for j in range(grid_rows):
        perm = []
        for c in range(grid_cols):
            s = c % grid_rows
            source_col = 4 * (j // 2) + 2 * (c // grid_rows) + j % 2
            perm.append((s * grid_cols + source_col, ((s + j) % grid_rows) * grid_cols + c))
        moved = lax.ppermute(piece, ("row", "col"), perm)
        mine = moved if mine is None else mine + moved
    ring = [mine]
    for step in range(1, grid_rows // 2):
        perm = [(i, (i + 2 * step) % grid_rows) for i in range(grid_rows)]
        ring.append(lax.ppermute(mine, "row", perm))
    ring = jnp.stack(ring)
    partner = lax.ppermute(ring, "row", [(i, i ^ 1) for i in range(grid_rows)])
    combined = jnp.concatenate([ring, partner], axis=0)
    chunk_ids = jnp.arange(grid_rows, dtype=jnp.int32)
    own_d = (my_row - src_row - chunk_ids) % grid_rows
    par_d = ((my_row ^ 1) - src_row - chunk_ids) % grid_rows
    pos = jnp.where(own_d % 2 == 0, own_d // 2, grid_rows // 2 + par_d // 2)
    col_factor = combined[pos].reshape(cols_dev, tile, lead_w)

    prod = jnp.einsum("aik,bjk->abij", factor_rows, col_factor, precision=PRECISE)
    schur = (current - prod).reshape((rows_dev * cols_dev,) + current.shape[2:])

    flat_idx = send_local[:, None] * cols_dev + col_local[None, :]
    keep = (send_valid[:, None] & col_valid[None, :])[:, :, None, None]
    outgoing = jnp.where(keep, schur[flat_idx], 0.0)
    incoming = lax.all_to_all(outgoing, "row", split_axis=0, concat_axis=0, tiled=True)
    parent = jnp.where(recv_valid[:, None, None, None], incoming[recv_source], 0.0)
    return (factor_rows[:, None], parent[:, None, :, None])


def solution(mesh):
    in_specs = (P(None, "row", None, "col", None, None), P(), P(), P())
    out_specs = (P(None, "row", None, None), P(None, "row", None, "col", None, None))
    return jax.shard_map(local, mesh=mesh, in_specs=in_specs, out_specs=out_specs, check_vma=False)
```

```python
import jax
import jax.numpy as jnp
from jax import lax
from jax.sharding import PartitionSpec as P

LEAD = 4
SCHUR_PRECISION = lax.Precision.HIGH


def valid_gain(valid_flags, ndims):
    return valid_flags.astype(jnp.float32).reshape((-1,) + (1,) * (ndims - 1))


def route_rows(block_now, send_local, send_valid, recv_source, recv_valid, grid_rows):
    outgoing = jnp.take(block_now, send_local, axis=0) * valid_gain(send_valid, block_now.ndim)
    outgoing = outgoing.reshape((grid_rows, -1) + block_now.shape[1:])
    incoming = lax.all_to_all(outgoing, "row", split_axis=0, concat_axis=0, tiled=True)
    incoming = incoming.reshape((-1,) + block_now.shape[1:])
    return jnp.take(incoming, recv_source, axis=0) * valid_gain(recv_valid, block_now.ndim)


def local(front, tile_live, row_target, col_target):
    grid_rows = lax.axis_size("row")
    grid_cols = lax.axis_size("col")
    my_row = lax.axis_index("row")
    my_col = lax.axis_index("col")
    rows_dev = front.shape[0]
    cols_dev = front.shape[2]
    tile = front.shape[4]
    lead_w = LEAD * tile
    per_dest = rows_dev // grid_rows
    current = front[:, 0, :, 0]
    update_count = tile_live.shape[0]

    update_index = jnp.arange(update_count, dtype=jnp.int32)
    source_row = (update_index + LEAD) % grid_rows
    target_row = row_target % grid_rows
    target_slot = row_target // grid_rows
    earlier = (
        (source_row[:, None] == source_row[None, :])
        & (target_row[:, None] == target_row[None, :])
        & (update_index[None, :] < update_index[:, None])
    )
    arrival = jnp.sum(earlier.astype(jnp.int32), axis=1)
    send_slots = jnp.arange(grid_rows * per_dest, dtype=jnp.int32)
    send_match = (
        (source_row[None, :] == my_row)
        & (target_row[None, :] == send_slots[:, None] // per_dest)
        & (arrival[None, :] == send_slots[:, None] % per_dest)
    ).astype(jnp.int32)
    send_local = jnp.sum(send_match * ((update_index + LEAD) // grid_rows)[None, :], axis=1)
    send_valid = jnp.sum(send_match, axis=1) > 0
    out_slots = jnp.arange(rows_dev, dtype=jnp.int32)
    recv_match = (
        (target_row[None, :] == my_row) & (target_slot[None, :] == out_slots[:, None])
    ).astype(jnp.int32)
    recv_source = jnp.sum(recv_match * (source_row * per_dest + arrival)[None, :], axis=1)
    recv_valid = jnp.sum(recv_match, axis=1) > 0
    source_col = (update_index + LEAD) % grid_cols
    out_cols = jnp.arange(cols_dev, dtype=jnp.int32)
    col_match = (
        (source_col[None, :] == my_col) & ((col_target // grid_cols)[None, :] == out_cols[:, None])
    ).astype(jnp.int32)
    col_local = jnp.sum(col_match * ((update_index + LEAD) // grid_cols)[None, :], axis=1)
    col_valid = jnp.sum(col_match, axis=1) > 0
    col_gain = col_valid.astype(jnp.float32)

    lead_tile = current[0, 0]
    row_tiles = lax.all_gather(lead_tile, "col")[:LEAD]
    lead_tiles = lax.all_gather(row_tiles, "row")[:LEAD]
    lead_block = lead_tiles.transpose(0, 2, 1, 3).reshape(lead_w, lead_w)
    chunks = rows_dev * 2
    half = tile // 2
    panel_col = current[:, 0].reshape(chunks, half, tile)
    gathered = lax.all_to_all(panel_col, "col", split_axis=0, concat_axis=0, tiled=True)
    panel_rows = gathered[:LEAD].transpose(1, 0, 2).reshape(half, lead_w)
    my_tile_row = (my_col // 2) * grid_rows + my_row
    live = jnp.where(
        my_tile_row >= LEAD,
        jnp.take(tile_live, jnp.clip(my_tile_row - LEAD, 0, update_count - 1)),
        1,
    ).astype(jnp.float32)
    masked = panel_rows * live
    bound = 1.0 + 10.0 * jnp.sum(masked * masked)
    aug = jnp.concatenate(
        [
            jnp.concatenate([lead_block, jnp.zeros((lead_w, half), jnp.float32)], axis=1),
            jnp.concatenate([masked, jnp.where(jnp.eye(half, dtype=jnp.bool_), bound, 0.0)], axis=1),
        ],
        axis=0,
    )
    aug_factor = lax.linalg.cholesky(aug, symmetrize_input=False)
    chol = aug_factor[:lead_w, :lead_w]
    solved = aug_factor[lead_w:, :lead_w]
    start = jnp.clip(my_tile_row * tile + (my_col % 2) * half, 0, lead_w - half)
    chol_rows = lax.dynamic_slice(chol, (start, 0), (half, lead_w))
    piece = jnp.where(my_tile_row < LEAD, chol_rows, solved)
    factor_rows = lax.all_gather(piece, "col").reshape(rows_dev, tile, lead_w)

    src_row = my_col % grid_rows
    mine = None
    for j in range(grid_rows):
        perm = []
        for c in range(grid_cols):
            s = c % grid_rows
            source_col = 4 * (j // 2) + 2 * (c // grid_rows) + j % 2
            perm.append((s * grid_cols + source_col, ((s + j) % grid_rows) * grid_cols + c))
        moved = lax.ppermute(piece, ("row", "col"), perm)
        mine = moved if mine is None else mine + moved
    ring = [mine]
    for step in range(1, grid_rows // 2):
        perm = [(i, (i + 2 * step) % grid_rows) for i in range(grid_rows)]
        ring.append(lax.ppermute(mine, "row", perm))
    ring = jnp.stack(ring)
    partner = lax.ppermute(ring, "row", [(i, i ^ 1) for i in range(grid_rows)])
    combined = jnp.concatenate([ring, partner], axis=0)
    chunk_ids = jnp.arange(grid_rows, dtype=jnp.int32)
    own_d = (my_row - src_row - chunk_ids) % grid_rows
    par_d = ((my_row ^ 1) - src_row - chunk_ids) % grid_rows
    pos = jnp.where(own_d % 2 == 0, own_d // 2, grid_rows // 2 + par_d // 2)
    col_factor = combined[pos].reshape(cols_dev, tile, lead_w)

    prod = lax.dot_general(
        factor_rows.reshape(rows_dev * tile, lead_w),
        col_factor.reshape(cols_dev * tile, lead_w),
        (((1,), (1,)), ((), ())),
        precision=SCHUR_PRECISION,
    )
    prod = prod.reshape(rows_dev, tile, cols_dev, tile).transpose(0, 2, 1, 3)
    schur = (current - prod).reshape((rows_dev * cols_dev,) + current.shape[2:])

    flat_idx = send_local[:, None] * cols_dev + col_local[None, :]
    keep = (send_valid[:, None] & col_valid[None, :])[:, :, None, None]
    outgoing = jnp.where(keep, schur[flat_idx], 0.0)
    incoming = lax.all_to_all(outgoing, "row", split_axis=0, concat_axis=0, tiled=True)
    parent = jnp.where(recv_valid[:, None, None, None], incoming[recv_source], 0.0)
    return (factor_rows[:, None], parent[:, None, :, None])


def solution(mesh):
    in_specs = (P(None, "row", None, "col", None, None), P(), P(), P())
    out_specs = (P(None, "row", None, None), P(None, "row", None, "col", None, None))
    return jax.shard_map(local, mesh=mesh, in_specs=in_specs, out_specs=out_specs, check_vma=False)
```

```python
import jax
import jax.numpy as jnp
from jax import lax
from jax.sharding import PartitionSpec as P

LEAD = 4
SCHUR_PRECISION = lax.Precision.HIGH


def valid_gain(valid_flags, ndims):
    return valid_flags.astype(jnp.float32).reshape((-1,) + (1,) * (ndims - 1))


def route_rows(block_now, send_local, send_valid, recv_source, recv_valid, grid_rows):
    outgoing = jnp.take(block_now, send_local, axis=0) * valid_gain(send_valid, block_now.ndim)
    outgoing = outgoing.reshape((grid_rows, -1) + block_now.shape[1:])
    incoming = lax.all_to_all(outgoing, "row", split_axis=0, concat_axis=0, tiled=True)
    incoming = incoming.reshape((-1,) + block_now.shape[1:])
    return jnp.take(incoming, recv_source, axis=0) * valid_gain(recv_valid, block_now.ndim)


def local(front, tile_live, row_target, col_target):
    grid_rows = lax.axis_size("row")
    grid_cols = lax.axis_size("col")
    my_row = lax.axis_index("row")
    my_col = lax.axis_index("col")
    rows_dev = front.shape[0]
    cols_dev = front.shape[2]
    tile = front.shape[4]
    lead_w = LEAD * tile
    per_dest = rows_dev // grid_rows
    current = front[:, 0, :, 0]
    update_count = tile_live.shape[0]

    update_index = jnp.arange(update_count, dtype=jnp.int32)
    source_row = (update_index + LEAD) % grid_rows
    target_row = row_target % grid_rows
    target_slot = row_target // grid_rows
    earlier = (
        (source_row[:, None] == source_row[None, :])
        & (target_row[:, None] == target_row[None, :])
        & (update_index[None, :] < update_index[:, None])
    )
    arrival = jnp.sum(earlier.astype(jnp.int32), axis=1)
    send_slots = jnp.arange(grid_rows * per_dest, dtype=jnp.int32)
    send_match = (
        (source_row[None, :] == my_row)
        & (target_row[None, :] == send_slots[:, None] // per_dest)
        & (arrival[None, :] == send_slots[:, None] % per_dest)
    ).astype(jnp.int32)
    send_local = jnp.sum(send_match * ((update_index + LEAD) // grid_rows)[None, :], axis=1)
    send_valid = jnp.sum(send_match, axis=1) > 0
    out_slots = jnp.arange(rows_dev, dtype=jnp.int32)
    recv_match = (
        (target_row[None, :] == my_row) & (target_slot[None, :] == out_slots[:, None])
    ).astype(jnp.int32)
    recv_source = jnp.sum(recv_match * (source_row * per_dest + arrival)[None, :], axis=1)
    recv_valid = jnp.sum(recv_match, axis=1) > 0
    source_col = (update_index + LEAD) % grid_cols
    out_cols = jnp.arange(cols_dev, dtype=jnp.int32)
    col_match = (
        (source_col[None, :] == my_col) & ((col_target // grid_cols)[None, :] == out_cols[:, None])
    ).astype(jnp.int32)
    col_local = jnp.sum(col_match * ((update_index + LEAD) // grid_cols)[None, :], axis=1)
    col_valid = jnp.sum(col_match, axis=1) > 0
    col_gain = col_valid.astype(jnp.float32)

    lead_tile = current[0, 0]
    row_tiles = lax.all_gather(lead_tile, "col")[:LEAD]
    lead_tiles = lax.all_gather(row_tiles, "row")[:LEAD]
    lead_block = lead_tiles.transpose(0, 2, 1, 3).reshape(lead_w, lead_w)
    chunks = rows_dev * 2
    half = tile // 2
    panel_col = current[:, 0].reshape(chunks, half, tile)
    gathered = lax.all_to_all(panel_col, "col", split_axis=0, concat_axis=0, tiled=True)
    panel_rows = gathered[:LEAD].transpose(1, 0, 2).reshape(half, lead_w)
    my_tile_row = (my_col // 2) * grid_rows + my_row
    live = jnp.where(
        my_tile_row >= LEAD,
        jnp.take(tile_live, jnp.clip(my_tile_row - LEAD, 0, update_count - 1)),
        1,
    ).astype(jnp.float32)
    masked = panel_rows * live
    bound = 1.0 + 10.0 * jnp.sum(masked * masked)
    aug = jnp.concatenate(
        [
            jnp.concatenate([lead_block, jnp.zeros((lead_w, half), jnp.float32)], axis=1),
            jnp.concatenate([masked, jnp.where(jnp.eye(half, dtype=jnp.bool_), bound, 0.0)], axis=1),
        ],
        axis=0,
    )
    aug_factor = lax.linalg.cholesky(aug, symmetrize_input=False)
    chol = aug_factor[:lead_w, :lead_w]
    solved = aug_factor[lead_w:, :lead_w]
    start = jnp.clip(my_tile_row * tile + (my_col % 2) * half, 0, lead_w - half)
    chol_rows = lax.dynamic_slice(chol, (start, 0), (half, lead_w))
    piece = jnp.where(my_tile_row < LEAD, chol_rows, solved)
    factor_rows = lax.all_gather(piece, "col").reshape(rows_dev, tile, lead_w)

    src_row = my_col % grid_rows
    mine = None
    for j in range(grid_rows):
        perm = []
        for c in range(grid_cols):
            s = c % grid_rows
            source_col = 4 * (j // 2) + 2 * (c // grid_rows) + j % 2
            perm.append((s * grid_cols + source_col, ((s + j) % grid_rows) * grid_cols + c))
        moved = lax.ppermute(piece, ("row", "col"), perm)
        mine = moved if mine is None else mine + moved
    ring = [mine]
    for step in range(1, grid_rows // 2):
        perm = [(i, (i + 2 * step) % grid_rows) for i in range(grid_rows)]
        ring.append(lax.ppermute(mine, "row", perm))
    ring = jnp.stack(ring)
    partner = lax.ppermute(ring, "row", [(i, i ^ 1) for i in range(grid_rows)])
    combined = jnp.concatenate([ring, partner], axis=0)
    chunk_ids = jnp.arange(grid_rows, dtype=jnp.int32)
    own_d = (my_row - src_row - chunk_ids) % grid_rows
    par_d = ((my_row ^ 1) - src_row - chunk_ids) % grid_rows
    pos = jnp.where(own_d % 2 == 0, own_d // 2, grid_rows // 2 + par_d // 2)
    col_factor = combined[pos].reshape(cols_dev, tile, lead_w)

    prod = lax.dot_general(
        factor_rows.reshape(rows_dev * tile, lead_w),
        col_factor.reshape(cols_dev * tile, lead_w),
        (((1,), (1,)), ((), ())),
        precision=SCHUR_PRECISION,
    )
    prod = prod.reshape(rows_dev, tile, cols_dev, tile).transpose(0, 2, 1, 3)
    schur = (current - prod).reshape((rows_dev * cols_dev,) + current.shape[2:])

    flat_idx = send_local[:, None] * cols_dev + col_local[None, :]
    outgoing = schur[flat_idx]
    incoming = lax.all_to_all(outgoing, "row", split_axis=0, concat_axis=0, tiled=True)
    keep = (recv_valid[:, None] & col_valid[None, :])[:, :, None, None]
    parent = jnp.where(keep, incoming[recv_source], 0.0)
    return (factor_rows[:, None], parent[:, None, :, None])


def solution(mesh):
    in_specs = (P(None, "row", None, "col", None, None), P(), P(), P())
    out_specs = (P(None, "row", None, None), P(None, "row", None, "col", None, None))
    return jax.shard_map(local, mesh=mesh, in_specs=in_specs, out_specs=out_specs, check_vma=False)
```

```python
import jax
import jax.numpy as jnp
from jax import lax
from jax.sharding import PartitionSpec as P

LEAD = 4
SCHUR_PRECISION = lax.Precision.HIGH
PRECISE = lax.Precision.HIGHEST


def valid_gain(valid_flags, ndims):
    return valid_flags.astype(jnp.float32).reshape((-1,) + (1,) * (ndims - 1))


def route_rows(block_now, send_local, send_valid, recv_source, recv_valid, grid_rows):
    outgoing = jnp.take(block_now, send_local, axis=0) * valid_gain(send_valid, block_now.ndim)
    outgoing = outgoing.reshape((grid_rows, -1) + block_now.shape[1:])
    incoming = lax.all_to_all(outgoing, "row", split_axis=0, concat_axis=0, tiled=True)
    incoming = incoming.reshape((-1,) + block_now.shape[1:])
    return jnp.take(incoming, recv_source, axis=0) * valid_gain(recv_valid, block_now.ndim)


def column_gather(piece, my_row, my_col, grid_rows, grid_cols):
    src_row = my_col % grid_rows
    mine = None
    for j in range(grid_rows):
        perm = []
        for c in range(grid_cols):
            s = c % grid_rows
            source_col = 4 * (j // 2) + 2 * (c // grid_rows) + j % 2
            perm.append((s * grid_cols + source_col, ((s + j) % grid_rows) * grid_cols + c))
        moved = lax.ppermute(piece, ("row", "col"), perm)
        mine = moved if mine is None else mine + moved
    ring = [mine]
    for step in range(1, grid_rows // 2):
        perm = [(i, (i + 2 * step) % grid_rows) for i in range(grid_rows)]
        ring.append(lax.ppermute(mine, "row", perm))
    ring = jnp.stack(ring)
    partner = lax.ppermute(ring, "row", [(i, i ^ 1) for i in range(grid_rows)])
    combined = jnp.concatenate([ring, partner], axis=0)
    chunk_ids = jnp.arange(grid_rows, dtype=jnp.int32)
    own_d = (my_row - src_row - chunk_ids) % grid_rows
    par_d = ((my_row ^ 1) - src_row - chunk_ids) % grid_rows
    pos = jnp.where(own_d % 2 == 0, own_d // 2, grid_rows // 2 + par_d // 2)
    return combined[pos].reshape(grid_rows * piece.shape[0], piece.shape[1])


def local(front, tile_live, row_target, col_target):
    grid_rows = lax.axis_size("row")
    grid_cols = lax.axis_size("col")
    my_row = lax.axis_index("row")
    my_col = lax.axis_index("col")
    rows_dev = front.shape[0]
    cols_dev = front.shape[2]
    tile = front.shape[4]
    lead_w = LEAD * tile
    per_dest = rows_dev // grid_rows
    current = front[:, 0, :, 0]
    update_count = tile_live.shape[0]

    update_index = jnp.arange(update_count, dtype=jnp.int32)
    source_row = (update_index + LEAD) % grid_rows
    target_row = row_target % grid_rows
    target_slot = row_target // grid_rows
    earlier = (
        (source_row[:, None] == source_row[None, :])
        & (target_row[:, None] == target_row[None, :])
        & (update_index[None, :] < update_index[:, None])
    )
    arrival = jnp.sum(earlier.astype(jnp.int32), axis=1)
    send_slots = jnp.arange(grid_rows * per_dest, dtype=jnp.int32)
    send_match = (
        (source_row[None, :] == my_row)
        & (target_row[None, :] == send_slots[:, None] // per_dest)
        & (arrival[None, :] == send_slots[:, None] % per_dest)
    ).astype(jnp.int32)
    send_local = jnp.sum(send_match * ((update_index + LEAD) // grid_rows)[None, :], axis=1)
    send_valid = jnp.sum(send_match, axis=1) > 0
    out_slots = jnp.arange(rows_dev, dtype=jnp.int32)
    recv_match = (
        (target_row[None, :] == my_row) & (target_slot[None, :] == out_slots[:, None])
    ).astype(jnp.int32)
    recv_source = jnp.sum(recv_match * (source_row * per_dest + arrival)[None, :], axis=1)
    recv_valid = jnp.sum(recv_match, axis=1) > 0
    source_col = (update_index + LEAD) % grid_cols
    out_cols = jnp.arange(cols_dev, dtype=jnp.int32)
    col_match = (
        (source_col[None, :] == my_col) & ((col_target // grid_cols)[None, :] == out_cols[:, None])
    ).astype(jnp.int32)
    col_local = jnp.sum(col_match * ((update_index + LEAD) // grid_cols)[None, :], axis=1)
    col_valid = jnp.sum(col_match, axis=1) > 0
    col_gain = col_valid.astype(jnp.float32)

    lead_tile = current[0, 0]
    row_tiles = lax.all_gather(lead_tile, "col")[:LEAD]
    lead_tiles = lax.all_gather(row_tiles, "row")[:LEAD]
    lead_block = lead_tiles.transpose(0, 2, 1, 3).reshape(lead_w, lead_w)
    chunks = rows_dev * 2
    half = tile // 2
    panel_col = current[:, 0].reshape(chunks, half, tile)
    gathered = lax.all_to_all(panel_col, "col", split_axis=0, concat_axis=0, tiled=True)
    panel_rows = gathered[:LEAD].transpose(1, 0, 2).reshape(half, lead_w)
    my_tile_row = (my_col // 2) * grid_rows + my_row
    live = jnp.where(
        my_tile_row >= LEAD,
        jnp.take(tile_live, jnp.clip(my_tile_row - LEAD, 0, update_count - 1)),
        1,
    ).astype(jnp.float32)
    masked = panel_rows * live
    block = 128
    groups = 4
    steps = lead_w // block
    work = jnp.concatenate([lead_block, masked], axis=0)
    row_start = jnp.clip(my_tile_row * tile + (my_col % 2) * half, 0, lead_w - half)
    use_chol = my_tile_row < LEAD
    blocks = []
    row_parts = []
    col_parts = []
    for k in range(steps):
        lo = k * block
        diag = lax.linalg.cholesky(work[lo:lo + block, lo:lo + block], symmetrize_input=False)
        below = lax.linalg.triangular_solve(
            diag, work[lo + block:, lo:lo + block], left_side=False, lower=True, transpose_a=True
        )
        if k + 1 < steps:
            upd = jnp.dot(below, below[: lead_w - lo - block].T, precision=PRECISE)
            work = work.at[lo + block:, lo + block:lead_w].add(-upd)
        column = jnp.concatenate([jnp.zeros((lo, block), jnp.float32), diag, below], axis=0)
        chol_rows = lax.dynamic_slice(column, (row_start, 0), (half, block))
        blocks.append(jnp.where(use_chol, chol_rows, column[lead_w:]))
        if (k + 1) % (steps // groups) == 0:
            piece = jnp.concatenate(blocks, axis=1)
            blocks = []
            row_parts.append(lax.all_gather(piece, "col").reshape(rows_dev * tile, -1))
            col_parts.append(column_gather(piece, my_row, my_col, grid_rows, grid_cols))
    factor_rows = jnp.concatenate(row_parts, axis=1).reshape(rows_dev, tile, lead_w)
    col_factor = jnp.concatenate(col_parts, axis=1).reshape(cols_dev, tile, lead_w)

    prod = lax.dot_general(
        factor_rows.reshape(rows_dev * tile, lead_w),
        col_factor.reshape(cols_dev * tile, lead_w),
        (((1,), (1,)), ((), ())),
        precision=SCHUR_PRECISION,
    )
    prod = prod.reshape(rows_dev, tile, cols_dev, tile).transpose(0, 2, 1, 3)
    schur = (current - prod).reshape((rows_dev * cols_dev,) + current.shape[2:])

    flat_idx = send_local[:, None] * cols_dev + col_local[None, :]
    outgoing = schur[flat_idx]
    incoming = lax.all_to_all(outgoing, "row", split_axis=0, concat_axis=0, tiled=True)
    keep = (recv_valid[:, None] & col_valid[None, :])[:, :, None, None]
    parent = jnp.where(keep, incoming[recv_source], 0.0)
    return (factor_rows[:, None], parent[:, None, :, None])


def solution(mesh):
    in_specs = (P(None, "row", None, "col", None, None), P(), P(), P())
    out_specs = (P(None, "row", None, None), P(None, "row", None, "col", None, None))
    return jax.shard_map(local, mesh=mesh, in_specs=in_specs, out_specs=out_specs, check_vma=False)
```

```python
import jax
import jax.numpy as jnp
from jax import lax
from jax.sharding import PartitionSpec as P

LEAD = 4
SCHUR_PRECISION = lax.Precision.HIGH
PRECISE = lax.Precision.HIGHEST


def valid_gain(valid_flags, ndims):
    return valid_flags.astype(jnp.float32).reshape((-1,) + (1,) * (ndims - 1))


def route_rows(block_now, send_local, send_valid, recv_source, recv_valid, grid_rows):
    outgoing = jnp.take(block_now, send_local, axis=0) * valid_gain(send_valid, block_now.ndim)
    outgoing = outgoing.reshape((grid_rows, -1) + block_now.shape[1:])
    incoming = lax.all_to_all(outgoing, "row", split_axis=0, concat_axis=0, tiled=True)
    incoming = incoming.reshape((-1,) + block_now.shape[1:])
    return jnp.take(incoming, recv_source, axis=0) * valid_gain(recv_valid, block_now.ndim)


def column_gather(piece, my_row, my_col, grid_rows, grid_cols):
    src_row = my_col % grid_rows
    mine = None
    for j in range(grid_rows):
        perm = []
        for c in range(grid_cols):
            s = c % grid_rows
            source_col = 4 * (j // 2) + 2 * (c // grid_rows) + j % 2
            perm.append((s * grid_cols + source_col, ((s + j) % grid_rows) * grid_cols + c))
        moved = lax.ppermute(piece, ("row", "col"), perm)
        mine = moved if mine is None else mine + moved
    ring = [mine]
    for step in range(1, grid_rows // 2):
        perm = [(i, (i + 2 * step) % grid_rows) for i in range(grid_rows)]
        ring.append(lax.ppermute(mine, "row", perm))
    ring = jnp.stack(ring)
    partner = lax.ppermute(ring, "row", [(i, i ^ 1) for i in range(grid_rows)])
    combined = jnp.concatenate([ring, partner], axis=0)
    chunk_ids = jnp.arange(grid_rows, dtype=jnp.int32)
    own_d = (my_row - src_row - chunk_ids) % grid_rows
    par_d = ((my_row ^ 1) - src_row - chunk_ids) % grid_rows
    pos = jnp.where(own_d % 2 == 0, own_d // 2, grid_rows // 2 + par_d // 2)
    return combined[pos].reshape(grid_rows * piece.shape[0], piece.shape[1])


def local(front, tile_live, row_target, col_target):
    grid_rows = lax.axis_size("row")
    grid_cols = lax.axis_size("col")
    my_row = lax.axis_index("row")
    my_col = lax.axis_index("col")
    rows_dev = front.shape[0]
    cols_dev = front.shape[2]
    tile = front.shape[4]
    lead_w = LEAD * tile
    per_dest = rows_dev // grid_rows
    current = front[:, 0, :, 0]
    update_count = tile_live.shape[0]

    update_index = jnp.arange(update_count, dtype=jnp.int32)
    source_row = (update_index + LEAD) % grid_rows
    target_row = row_target % grid_rows
    target_slot = row_target // grid_rows
    earlier = (
        (source_row[:, None] == source_row[None, :])
        & (target_row[:, None] == target_row[None, :])
        & (update_index[None, :] < update_index[:, None])
    )
    arrival = jnp.sum(earlier.astype(jnp.int32), axis=1)
    send_slots = jnp.arange(grid_rows * per_dest, dtype=jnp.int32)
    send_match = (
        (source_row[None, :] == my_row)
        & (target_row[None, :] == send_slots[:, None] // per_dest)
        & (arrival[None, :] == send_slots[:, None] % per_dest)
    ).astype(jnp.int32)
    send_local = jnp.sum(send_match * ((update_index + LEAD) // grid_rows)[None, :], axis=1)
    send_valid = jnp.sum(send_match, axis=1) > 0
    out_slots = jnp.arange(rows_dev, dtype=jnp.int32)
    recv_match = (
        (target_row[None, :] == my_row) & (target_slot[None, :] == out_slots[:, None])
    ).astype(jnp.int32)
    recv_source = jnp.sum(recv_match * (source_row * per_dest + arrival)[None, :], axis=1)
    recv_valid = jnp.sum(recv_match, axis=1) > 0
    source_col = (update_index + LEAD) % grid_cols
    out_cols = jnp.arange(cols_dev, dtype=jnp.int32)
    col_match = (
        (source_col[None, :] == my_col) & ((col_target // grid_cols)[None, :] == out_cols[:, None])
    ).astype(jnp.int32)
    col_local = jnp.sum(col_match * ((update_index + LEAD) // grid_cols)[None, :], axis=1)
    col_valid = jnp.sum(col_match, axis=1) > 0
    col_gain = col_valid.astype(jnp.float32)

    lead_tile = current[0, 0]
    row_tiles = lax.all_gather(lead_tile, "col")[:LEAD]
    lead_tiles = lax.all_gather(row_tiles, "row")[:LEAD]
    lead_block = lead_tiles.transpose(0, 2, 1, 3).reshape(lead_w, lead_w)
    chunks = rows_dev * 2
    half = tile // 2
    panel_col = current[:, 0].reshape(chunks, half, tile)
    gathered = lax.all_to_all(panel_col, "col", split_axis=0, concat_axis=0, tiled=True)
    panel_rows = gathered[:LEAD].transpose(1, 0, 2).reshape(half, lead_w)
    my_tile_row = (my_col // 2) * grid_rows + my_row
    live = jnp.where(
        my_tile_row >= LEAD,
        jnp.take(tile_live, jnp.clip(my_tile_row - LEAD, 0, update_count - 1)),
        1,
    ).astype(jnp.float32)
    masked = panel_rows * live
    block = 128
    groups = 4
    steps = lead_w // block
    work = jnp.concatenate([lead_block, masked], axis=0)
    row_start = jnp.clip(my_tile_row * tile + (my_col % 2) * half, 0, lead_w - half)
    use_chol = my_tile_row < LEAD
    blocks = []
    row_parts = []
    col_parts = []
    for k in range(steps):
        lo = k * block
        diag = lax.linalg.cholesky(work[lo:lo + block, lo:lo + block], symmetrize_input=False)
        below = lax.linalg.triangular_solve(
            diag, work[lo + block:, lo:lo + block], left_side=False, lower=True, transpose_a=True
        )
        if k + 1 < steps:
            upd = jnp.dot(below, below[: lead_w - lo - block].T, precision=PRECISE)
            work = work.at[lo + block:, lo + block:lead_w].add(-upd)
        column = jnp.concatenate([jnp.zeros((lo, block), jnp.float32), diag, below], axis=0)
        chol_rows = lax.dynamic_slice(column, (row_start, 0), (half, block))
        blocks.append(jnp.where(use_chol, chol_rows, column[lead_w:]))
        if (k + 1) % (steps // groups) == 0:
            piece = jnp.concatenate(blocks, axis=1)
            blocks = []
            row_parts.append(lax.all_gather(piece, "col").reshape(rows_dev * tile, -1))
            col_parts.append(column_gather(piece, my_row, my_col, grid_rows, grid_cols))
    factor_rows = jnp.concatenate(row_parts, axis=1).reshape(rows_dev, tile, lead_w)

    prod = None
    for left, right in zip(row_parts, col_parts):
        term = lax.dot_general(
            left, right, (((1,), (1,)), ((), ())), precision=SCHUR_PRECISION
        )
        prod = term if prod is None else prod + term
    prod = prod.reshape(rows_dev, tile, cols_dev, tile).transpose(0, 2, 1, 3)
    schur = (current - prod).reshape((rows_dev * cols_dev,) + current.shape[2:])

    flat_idx = send_local[:, None] * cols_dev + col_local[None, :]
    outgoing = schur[flat_idx]
    incoming = lax.all_to_all(outgoing, "row", split_axis=0, concat_axis=0, tiled=True)
    keep = (recv_valid[:, None] & col_valid[None, :])[:, :, None, None]
    parent = jnp.where(keep, incoming[recv_source], 0.0)
    return (factor_rows[:, None], parent[:, None, :, None])


def solution(mesh):
    in_specs = (P(None, "row", None, "col", None, None), P(), P(), P())
    out_specs = (P(None, "row", None, None), P(None, "row", None, "col", None, None))
    return jax.shard_map(local, mesh=mesh, in_specs=in_specs, out_specs=out_specs, check_vma=False)
```

```python
import jax
import jax.numpy as jnp
from jax import lax
from jax.sharding import PartitionSpec as P

LEAD = 4
SCHUR_PRECISION = lax.Precision.HIGH


def valid_gain(valid_flags, ndims):
    return valid_flags.astype(jnp.float32).reshape((-1,) + (1,) * (ndims - 1))


def route_rows(block_now, send_local, send_valid, recv_source, recv_valid, grid_rows):
    outgoing = jnp.take(block_now, send_local, axis=0) * valid_gain(send_valid, block_now.ndim)
    outgoing = outgoing.reshape((grid_rows, -1) + block_now.shape[1:])
    incoming = lax.all_to_all(outgoing, "row", split_axis=0, concat_axis=0, tiled=True)
    incoming = incoming.reshape((-1,) + block_now.shape[1:])
    return jnp.take(incoming, recv_source, axis=0) * valid_gain(recv_valid, block_now.ndim)


def local(front, tile_live, row_target, col_target):
    grid_rows = lax.axis_size("row")
    grid_cols = lax.axis_size("col")
    my_row = lax.axis_index("row")
    my_col = lax.axis_index("col")
    rows_dev = front.shape[0]
    cols_dev = front.shape[2]
    tile = front.shape[4]
    lead_w = LEAD * tile
    per_dest = rows_dev // grid_rows
    current = front[:, 0, :, 0]
    update_count = tile_live.shape[0]

    update_index = jnp.arange(update_count, dtype=jnp.int32)
    source_row = (update_index + LEAD) % grid_rows
    target_row = row_target % grid_rows
    target_slot = row_target // grid_rows
    earlier = (
        (source_row[:, None] == source_row[None, :])
        & (target_row[:, None] == target_row[None, :])
        & (update_index[None, :] < update_index[:, None])
    )
    arrival = jnp.sum(earlier.astype(jnp.int32), axis=1)
    send_slots = jnp.arange(grid_rows * per_dest, dtype=jnp.int32)
    send_match = (
        (source_row[None, :] == my_row)
        & (target_row[None, :] == send_slots[:, None] // per_dest)
        & (arrival[None, :] == send_slots[:, None] % per_dest)
    ).astype(jnp.int32)
    send_local = jnp.sum(send_match * ((update_index + LEAD) // grid_rows)[None, :], axis=1)
    send_valid = jnp.sum(send_match, axis=1) > 0
    out_slots = jnp.arange(rows_dev, dtype=jnp.int32)
    recv_match = (
        (target_row[None, :] == my_row) & (target_slot[None, :] == out_slots[:, None])
    ).astype(jnp.int32)
    recv_source = jnp.sum(recv_match * (source_row * per_dest + arrival)[None, :], axis=1)
    recv_valid = jnp.sum(recv_match, axis=1) > 0
    source_col = (update_index + LEAD) % grid_cols
    out_cols = jnp.arange(cols_dev, dtype=jnp.int32)
    col_match = (
        (source_col[None, :] == my_col) & ((col_target // grid_cols)[None, :] == out_cols[:, None])
    ).astype(jnp.int32)
    col_local = jnp.sum(col_match * ((update_index + LEAD) // grid_cols)[None, :], axis=1)
    col_valid = jnp.sum(col_match, axis=1) > 0
    col_gain = col_valid.astype(jnp.float32)

    lead_tile = current[0, 0]
    slab = tile // grid_rows
    lead_slabs = lead_tile.reshape(grid_rows, slab, tile)
    held = None
    for r in range(grid_rows):
        perm = [
            (i * grid_cols + j, r * grid_cols + LEAD * i + j) for i in range(LEAD) for j in range(LEAD)
        ]
        moved = lax.ppermute(lead_slabs[r], ("row", "col"), perm)
        held = moved if held is None else held + moved
    everything = lax.all_gather(held, ("row", "col"))
    lead_tiles = everything.reshape(grid_rows, LEAD, LEAD, slab, tile)[:, :, :, :, :]
    lead_block = lead_tiles.transpose(1, 0, 3, 2, 4).reshape(lead_w, lead_w)
    chunks = rows_dev * 2
    half = tile // 2
    panel_col = current[:, 0].reshape(chunks, half, tile)
    gathered = lax.all_to_all(panel_col, "col", split_axis=0, concat_axis=0, tiled=True)
    panel_rows = gathered[:LEAD].transpose(1, 0, 2).reshape(half, lead_w)
    my_tile_row = (my_col // 2) * grid_rows + my_row
    live = jnp.where(
        my_tile_row >= LEAD,
        jnp.take(tile_live, jnp.clip(my_tile_row - LEAD, 0, update_count - 1)),
        1,
    ).astype(jnp.float32)
    masked = panel_rows * live
    bound = 1.0 + 10.0 * jnp.sum(masked * masked)
    aug = jnp.concatenate(
        [
            jnp.concatenate([lead_block, jnp.zeros((lead_w, half), jnp.float32)], axis=1),
            jnp.concatenate([masked, jnp.where(jnp.eye(half, dtype=jnp.bool_), bound, 0.0)], axis=1),
        ],
        axis=0,
    )
    aug_factor = lax.linalg.cholesky(aug, symmetrize_input=False)
    chol = aug_factor[:lead_w, :lead_w]
    solved = aug_factor[lead_w:, :lead_w]
    start = jnp.clip(my_tile_row * tile + (my_col % 2) * half, 0, lead_w - half)
    chol_rows = lax.dynamic_slice(chol, (start, 0), (half, lead_w))
    piece = jnp.where(my_tile_row < LEAD, chol_rows, solved)
    factor_rows = lax.all_gather(piece, "col").reshape(rows_dev, tile, lead_w)

    src_row = my_col % grid_rows
    mine = None
    for j in range(grid_rows):
        perm = []
        for c in range(grid_cols):
            s = c % grid_rows
            source_col = 4 * (j // 2) + 2 * (c // grid_rows) + j % 2
            perm.append((s * grid_cols + source_col, ((s + j) % grid_rows) * grid_cols + c))
        moved = lax.ppermute(piece, ("row", "col"), perm)
        mine = moved if mine is None else mine + moved
    ring = [mine]
    for step in range(1, grid_rows // 2):
        perm = [(i, (i + 2 * step) % grid_rows) for i in range(grid_rows)]
        ring.append(lax.ppermute(mine, "row", perm))
    ring = jnp.stack(ring)
    partner = lax.ppermute(ring, "row", [(i, i ^ 1) for i in range(grid_rows)])
    combined = jnp.concatenate([ring, partner], axis=0)
    chunk_ids = jnp.arange(grid_rows, dtype=jnp.int32)
    own_d = (my_row - src_row - chunk_ids) % grid_rows
    par_d = ((my_row ^ 1) - src_row - chunk_ids) % grid_rows
    pos = jnp.where(own_d % 2 == 0, own_d // 2, grid_rows // 2 + par_d // 2)
    col_factor = combined[pos].reshape(cols_dev, tile, lead_w)

    prod = lax.dot_general(
        factor_rows.reshape(rows_dev * tile, lead_w),
        col_factor.reshape(cols_dev * tile, lead_w),
        (((1,), (1,)), ((), ())),
        precision=SCHUR_PRECISION,
    )
    prod = prod.reshape(rows_dev, tile, cols_dev, tile).transpose(0, 2, 1, 3)
    schur = (current - prod).reshape((rows_dev * cols_dev,) + current.shape[2:])

    flat_idx = send_local[:, None] * cols_dev + col_local[None, :]
    outgoing = schur[flat_idx]
    incoming = lax.all_to_all(outgoing, "row", split_axis=0, concat_axis=0, tiled=True)
    keep = (recv_valid[:, None] & col_valid[None, :])[:, :, None, None]
    parent = jnp.where(keep, incoming[recv_source], 0.0)
    return (factor_rows[:, None], parent[:, None, :, None])


def solution(mesh):
    in_specs = (P(None, "row", None, "col", None, None), P(), P(), P())
    out_specs = (P(None, "row", None, None), P(None, "row", None, "col", None, None))
    return jax.shard_map(local, mesh=mesh, in_specs=in_specs, out_specs=out_specs, check_vma=False)
```

```python
import jax
import jax.numpy as jnp
from jax import lax
from jax.sharding import PartitionSpec as P

LEAD = 4
SCHUR_PRECISION = lax.Precision.HIGH


def valid_gain(valid_flags, ndims):
    return valid_flags.astype(jnp.float32).reshape((-1,) + (1,) * (ndims - 1))


def route_rows(block_now, send_local, send_valid, recv_source, recv_valid, grid_rows):
    outgoing = jnp.take(block_now, send_local, axis=0) * valid_gain(send_valid, block_now.ndim)
    outgoing = outgoing.reshape((grid_rows, -1) + block_now.shape[1:])
    incoming = lax.all_to_all(outgoing, "row", split_axis=0, concat_axis=0, tiled=True)
    incoming = incoming.reshape((-1,) + block_now.shape[1:])
    return jnp.take(incoming, recv_source, axis=0) * valid_gain(recv_valid, block_now.ndim)


def local(front, tile_live, row_target, col_target):
    grid_rows = lax.axis_size("row")
    grid_cols = lax.axis_size("col")
    my_row = lax.axis_index("row")
    my_col = lax.axis_index("col")
    rows_dev = front.shape[0]
    cols_dev = front.shape[2]
    tile = front.shape[4]
    lead_w = LEAD * tile
    per_dest = rows_dev // grid_rows
    current = front[:, 0, :, 0]
    update_count = tile_live.shape[0]

    update_index = jnp.arange(update_count, dtype=jnp.int32)
    source_row = (update_index + LEAD) % grid_rows
    target_row = row_target % grid_rows
    target_slot = row_target // grid_rows
    earlier = (
        (source_row[:, None] == source_row[None, :])
        & (target_row[:, None] == target_row[None, :])
        & (update_index[None, :] < update_index[:, None])
    )
    arrival = jnp.sum(earlier.astype(jnp.int32), axis=1)
    send_slots = jnp.arange(grid_rows * per_dest, dtype=jnp.int32)
    send_match = (
        (source_row[None, :] == my_row)
        & (target_row[None, :] == send_slots[:, None] // per_dest)
        & (arrival[None, :] == send_slots[:, None] % per_dest)
    ).astype(jnp.int32)
    send_local = jnp.sum(send_match * ((update_index + LEAD) // grid_rows)[None, :], axis=1)
    send_valid = jnp.sum(send_match, axis=1) > 0
    out_slots = jnp.arange(rows_dev, dtype=jnp.int32)
    recv_match = (
        (target_row[None, :] == my_row) & (target_slot[None, :] == out_slots[:, None])
    ).astype(jnp.int32)
    recv_source = jnp.sum(recv_match * (source_row * per_dest + arrival)[None, :], axis=1)
    recv_valid = jnp.sum(recv_match, axis=1) > 0
    source_col = (update_index + LEAD) % grid_cols
    out_cols = jnp.arange(cols_dev, dtype=jnp.int32)
    col_match = (
        (source_col[None, :] == my_col) & ((col_target // grid_cols)[None, :] == out_cols[:, None])
    ).astype(jnp.int32)
    col_local = jnp.sum(col_match * ((update_index + LEAD) // grid_cols)[None, :], axis=1)
    col_valid = jnp.sum(col_match, axis=1) > 0
    col_gain = col_valid.astype(jnp.float32)

    lead_tile = current[0, 0]
    slab = tile // grid_rows
    lead_slabs = lead_tile.reshape(grid_rows, slab, tile)
    held = None
    for r in range(grid_rows):
        perm = [
            (i * grid_cols + j, r * grid_cols + LEAD * i + j) for i in range(LEAD) for j in range(LEAD)
        ]
        moved = lax.ppermute(lead_slabs[r], ("row", "col"), perm)
        held = moved if held is None else held + moved
    everything = lax.all_gather(held, ("row", "col"))
    lead_tiles = everything.reshape(grid_rows, LEAD, LEAD, slab, tile)[:, :, :, :, :]
    lead_block = lead_tiles.transpose(1, 0, 3, 2, 4).reshape(lead_w, lead_w)
    chunks = rows_dev * 2
    half = tile // 2
    panel_col = current[:, 0].reshape(chunks, half, tile)
    gathered = lax.all_to_all(panel_col, "col", split_axis=0, concat_axis=0, tiled=True)
    panel_rows = gathered[:LEAD].transpose(1, 0, 2).reshape(half, lead_w)
    my_tile_row = (my_col // 2) * grid_rows + my_row
    live = jnp.where(
        my_tile_row >= LEAD,
        jnp.take(tile_live, jnp.clip(my_tile_row - LEAD, 0, update_count - 1)),
        1,
    ).astype(jnp.float32)
    masked = panel_rows * live
    bound = 1.0 + 10.0 * jnp.sum(masked * masked)
    aug = jnp.concatenate(
        [
            jnp.concatenate([lead_block, jnp.zeros((lead_w, half), jnp.float32)], axis=1),
            jnp.concatenate([masked, jnp.where(jnp.eye(half, dtype=jnp.bool_), bound, 0.0)], axis=1),
        ],
        axis=0,
    )
    aug_factor = lax.linalg.cholesky(aug, symmetrize_input=False)
    chol = aug_factor[:lead_w, :lead_w]
    solved = aug_factor[lead_w:, :lead_w]
    start = jnp.clip(my_tile_row * tile + (my_col % 2) * half, 0, lead_w - half)
    chol_rows = lax.dynamic_slice(chol, (start, 0), (half, lead_w))
    piece = jnp.where(my_tile_row < LEAD, chol_rows, solved)
    factor_rows = lax.all_gather(piece, "col").reshape(rows_dev, tile, lead_w)

    src_row = my_col % grid_rows
    mine = None
    for j in range(grid_rows):
        perm = []
        for c in range(grid_cols):
            s = c % grid_rows
            source_col = 4 * (j // 2) + 2 * (c // grid_rows) + j % 2
            perm.append((s * grid_cols + source_col, ((s + j) % grid_rows) * grid_cols + c))
        moved = lax.ppermute(piece, ("row", "col"), perm)
        mine = moved if mine is None else mine + moved
    ring = [mine]
    for step in range(1, grid_rows // 2):
        perm = [(i, (i + 2 * step) % grid_rows) for i in range(grid_rows)]
        ring.append(lax.ppermute(mine, "row", perm))
    ring = jnp.stack(ring)
    partner = lax.ppermute(ring, "row", [(i, i ^ 1) for i in range(grid_rows)])
    combined = jnp.concatenate([ring, partner], axis=0)
    chunk_ids = jnp.arange(grid_rows, dtype=jnp.int32)
    own_d = (my_row - src_row - chunk_ids) % grid_rows
    par_d = ((my_row ^ 1) - src_row - chunk_ids) % grid_rows
    pos = jnp.where(own_d % 2 == 0, own_d // 2, grid_rows // 2 + par_d // 2)
    col_factor = combined[pos].reshape(cols_dev, tile, lead_w)

    prod = lax.dot_general(
        factor_rows.reshape(rows_dev * tile, lead_w),
        col_factor.reshape(cols_dev * tile, lead_w),
        (((1,), (1,)), ((), ())),
        precision=SCHUR_PRECISION,
    )
    prod = prod.reshape(rows_dev, tile, cols_dev, tile).transpose(0, 2, 1, 3)
    schur = (current - prod).reshape((rows_dev * cols_dev,) + current.shape[2:])

    flat_idx = send_local[:, None] * cols_dev + col_local[None, :]
    outgoing = schur[flat_idx]
    incoming = lax.all_to_all(outgoing, "row", split_axis=0, concat_axis=0, tiled=True)
    keep = (recv_valid[:, None] & col_valid[None, :])[:, :, None, None]
    parent = jnp.stack(
        [
            jnp.where(keep[slot], lax.dynamic_index_in_dim(incoming, recv_source[slot], keepdims=False), 0.0)
            for slot in range(rows_dev)
        ]
    )
    return (factor_rows[:, None], parent[:, None, :, None])


def solution(mesh):
    in_specs = (P(None, "row", None, "col", None, None), P(), P(), P())
    out_specs = (P(None, "row", None, None), P(None, "row", None, "col", None, None))
    return jax.shard_map(local, mesh=mesh, in_specs=in_specs, out_specs=out_specs, check_vma=False)
```

```python
import jax
import jax.numpy as jnp
from jax import lax
from jax.sharding import PartitionSpec as P

LEAD = 4
SCHUR_PRECISION = lax.Precision.HIGH


def valid_gain(valid_flags, ndims):
    return valid_flags.astype(jnp.float32).reshape((-1,) + (1,) * (ndims - 1))


def route_rows(block_now, send_local, send_valid, recv_source, recv_valid, grid_rows):
    outgoing = jnp.take(block_now, send_local, axis=0) * valid_gain(send_valid, block_now.ndim)
    outgoing = outgoing.reshape((grid_rows, -1) + block_now.shape[1:])
    incoming = lax.all_to_all(outgoing, "row", split_axis=0, concat_axis=0, tiled=True)
    incoming = incoming.reshape((-1,) + block_now.shape[1:])
    return jnp.take(incoming, recv_source, axis=0) * valid_gain(recv_valid, block_now.ndim)


def local(front, tile_live, row_target, col_target):
    grid_rows = lax.axis_size("row")
    grid_cols = lax.axis_size("col")
    my_row = lax.axis_index("row")
    my_col = lax.axis_index("col")
    rows_dev = front.shape[0]
    cols_dev = front.shape[2]
    tile = front.shape[4]
    lead_w = LEAD * tile
    per_dest = rows_dev // grid_rows
    current = front[:, 0, :, 0]
    update_count = tile_live.shape[0]

    update_index = jnp.arange(update_count, dtype=jnp.int32)
    source_row = (update_index + LEAD) % grid_rows
    target_row = row_target % grid_rows
    target_slot = row_target // grid_rows
    earlier = (
        (source_row[:, None] == source_row[None, :])
        & (target_row[:, None] == target_row[None, :])
        & (update_index[None, :] < update_index[:, None])
    )
    arrival = jnp.sum(earlier.astype(jnp.int32), axis=1)
    send_slots = jnp.arange(grid_rows * per_dest, dtype=jnp.int32)
    send_match = (
        (source_row[None, :] == my_row)
        & (target_row[None, :] == send_slots[:, None] // per_dest)
        & (arrival[None, :] == send_slots[:, None] % per_dest)
    ).astype(jnp.int32)
    send_local = jnp.sum(send_match * ((update_index + LEAD) // grid_rows)[None, :], axis=1)
    send_valid = jnp.sum(send_match, axis=1) > 0
    out_slots = jnp.arange(rows_dev, dtype=jnp.int32)
    recv_match = (
        (target_row[None, :] == my_row) & (target_slot[None, :] == out_slots[:, None])
    ).astype(jnp.int32)
    recv_source = jnp.sum(recv_match * (source_row * per_dest + arrival)[None, :], axis=1)
    recv_valid = jnp.sum(recv_match, axis=1) > 0
    source_col = (update_index + LEAD) % grid_cols
    out_cols = jnp.arange(cols_dev, dtype=jnp.int32)
    col_match = (
        (source_col[None, :] == my_col) & ((col_target // grid_cols)[None, :] == out_cols[:, None])
    ).astype(jnp.int32)
    col_local = jnp.sum(col_match * ((update_index + LEAD) // grid_cols)[None, :], axis=1)
    col_valid = jnp.sum(col_match, axis=1) > 0
    col_gain = col_valid.astype(jnp.float32)

    lead_tile = current[0, 0]
    slab = tile // grid_rows
    lead_slabs = lead_tile.reshape(grid_rows, slab, tile)
    held = None
    for r in range(grid_rows):
        perm = [
            (i * grid_cols + j, r * grid_cols + LEAD * i + j) for i in range(LEAD) for j in range(LEAD)
        ]
        moved = lax.ppermute(lead_slabs[r], ("row", "col"), perm)
        held = moved if held is None else held + moved
    everything = lax.all_gather(held, ("row", "col"))
    lead_tiles = everything.reshape(grid_rows, LEAD, LEAD, slab, tile)[:, :, :, :, :]
    lead_block = lead_tiles.transpose(1, 0, 3, 2, 4).reshape(lead_w, lead_w)
    chunks = rows_dev * 2
    half = tile // 2
    panel_col = current[:, 0].reshape(chunks, half, tile)
    gathered = lax.all_to_all(panel_col, "col", split_axis=0, concat_axis=0, tiled=True)
    panel_rows = gathered[:LEAD].transpose(1, 0, 2).reshape(half, lead_w)
    my_tile_row = (my_col // 2) * grid_rows + my_row
    live = jnp.where(
        my_tile_row >= LEAD,
        jnp.take(tile_live, jnp.clip(my_tile_row - LEAD, 0, update_count - 1)),
        1,
    ).astype(jnp.float32)
    masked = panel_rows * live
    bound = 1.0 + 10.0 * jnp.sum(masked * masked)
    aug = jnp.concatenate(
        [
            jnp.concatenate([lead_block, jnp.zeros((lead_w, half), jnp.float32)], axis=1),
            jnp.concatenate([masked, jnp.where(jnp.eye(half, dtype=jnp.bool_), bound, 0.0)], axis=1),
        ],
        axis=0,
    )
    aug_factor = lax.linalg.cholesky(aug, symmetrize_input=False)
    chol = aug_factor[:lead_w, :lead_w]
    solved = aug_factor[lead_w:, :lead_w]
    start = jnp.clip(my_tile_row * tile + (my_col % 2) * half, 0, lead_w - half)
    chol_rows = lax.dynamic_slice(chol, (start, 0), (half, lead_w))
    piece = jnp.where(my_tile_row < LEAD, chol_rows, solved)
    factor_rows = lax.all_gather(piece, "col").reshape(rows_dev, tile, lead_w)

    src_row = my_col % grid_rows
    mine = None
    for j in range(grid_rows):
        perm = []
        for c in range(grid_cols):
            s = c % grid_rows
            source_col = 4 * (j // 2) + 2 * (c // grid_rows) + j % 2
            perm.append((s * grid_cols + source_col, ((s + j) % grid_rows) * grid_cols + c))
        moved = lax.ppermute(piece, ("row", "col"), perm)
        mine = moved if mine is None else mine + moved
    ring = [mine]
    for step in range(1, grid_rows // 2):
        perm = [(i, (i + 2 * step) % grid_rows) for i in range(grid_rows)]
        ring.append(lax.ppermute(mine, "row", perm))
    ring = jnp.stack(ring)
    partner = lax.ppermute(ring, "row", [(i, i ^ 1) for i in range(grid_rows)])
    combined = jnp.concatenate([ring, partner], axis=0)
    chunk_ids = jnp.arange(grid_rows, dtype=jnp.int32)
    own_d = (my_row - src_row - chunk_ids) % grid_rows
    par_d = ((my_row ^ 1) - src_row - chunk_ids) % grid_rows
    pos = jnp.where(own_d % 2 == 0, own_d // 2, grid_rows // 2 + par_d // 2)
    col_factor = combined[pos].reshape(cols_dev, tile, lead_w)

    col_sorted = col_factor[col_local].reshape(cols_dev * tile, lead_w)
    rows_out = []
    for slot in range(rows_dev):
        src = send_local[slot]
        left = lax.dynamic_index_in_dim(factor_rows, src, keepdims=False)
        prod = lax.dot_general(
            left, col_sorted, (((1,), (1,)), ((), ())), precision=SCHUR_PRECISION
        ).reshape(tile, cols_dev, tile).transpose(1, 0, 2)
        front_row = lax.dynamic_index_in_dim(current, src, keepdims=False)[col_local]
        rows_out.append(front_row - prod)
    outgoing = jnp.stack(rows_out)
    incoming = lax.all_to_all(outgoing, "row", split_axis=0, concat_axis=0, tiled=True)
    keep = (recv_valid[:, None] & col_valid[None, :])[:, :, None, None]
    parent = jnp.stack(
        [
            jnp.where(keep[slot], lax.dynamic_index_in_dim(incoming, recv_source[slot], keepdims=False), 0.0)
            for slot in range(rows_dev)
        ]
    )
    return (factor_rows[:, None], parent[:, None, :, None])


def solution(mesh):
    in_specs = (P(None, "row", None, "col", None, None), P(), P(), P())
    out_specs = (P(None, "row", None, None), P(None, "row", None, "col", None, None))
    return jax.shard_map(local, mesh=mesh, in_specs=in_specs, out_specs=out_specs, check_vma=False)
```

```python
import jax
import jax.numpy as jnp
from jax import lax
from jax.sharding import PartitionSpec as P

LEAD = 4
SCHUR_PRECISION = lax.Precision.HIGH


def valid_gain(valid_flags, ndims):
    return valid_flags.astype(jnp.float32).reshape((-1,) + (1,) * (ndims - 1))


def route_rows(block_now, send_local, send_valid, recv_source, recv_valid, grid_rows):
    outgoing = jnp.take(block_now, send_local, axis=0) * valid_gain(send_valid, block_now.ndim)
    outgoing = outgoing.reshape((grid_rows, -1) + block_now.shape[1:])
    incoming = lax.all_to_all(outgoing, "row", split_axis=0, concat_axis=0, tiled=True)
    incoming = incoming.reshape((-1,) + block_now.shape[1:])
    return jnp.take(incoming, recv_source, axis=0) * valid_gain(recv_valid, block_now.ndim)


def local(front, tile_live, row_target, col_target):
    grid_rows = lax.axis_size("row")
    grid_cols = lax.axis_size("col")
    my_row = lax.axis_index("row")
    my_col = lax.axis_index("col")
    rows_dev = front.shape[0]
    cols_dev = front.shape[2]
    tile = front.shape[4]
    lead_w = LEAD * tile
    per_dest = rows_dev // grid_rows
    current = front[:, 0, :, 0]
    update_count = tile_live.shape[0]

    update_index = jnp.arange(update_count, dtype=jnp.int32)
    source_row = (update_index + LEAD) % grid_rows
    target_row = row_target % grid_rows
    target_slot = row_target // grid_rows
    earlier = (
        (source_row[:, None] == source_row[None, :])
        & (target_row[:, None] == target_row[None, :])
        & (update_index[None, :] < update_index[:, None])
    )
    arrival = jnp.sum(earlier.astype(jnp.int32), axis=1)
    send_slots = jnp.arange(grid_rows * per_dest, dtype=jnp.int32)
    send_match = (
        (source_row[None, :] == my_row)
        & (target_row[None, :] == send_slots[:, None] // per_dest)
        & (arrival[None, :] == send_slots[:, None] % per_dest)
    ).astype(jnp.int32)
    send_local = jnp.sum(send_match * ((update_index + LEAD) // grid_rows)[None, :], axis=1)
    send_valid = jnp.sum(send_match, axis=1) > 0
    out_slots = jnp.arange(rows_dev, dtype=jnp.int32)
    recv_match = (
        (target_row[None, :] == my_row) & (target_slot[None, :] == out_slots[:, None])
    ).astype(jnp.int32)
    recv_source = jnp.sum(recv_match * (source_row * per_dest + arrival)[None, :], axis=1)
    recv_valid = jnp.sum(recv_match, axis=1) > 0
    source_col = (update_index + LEAD) % grid_cols
    out_cols = jnp.arange(cols_dev, dtype=jnp.int32)
    col_match = (
        (source_col[None, :] == my_col) & ((col_target // grid_cols)[None, :] == out_cols[:, None])
    ).astype(jnp.int32)
    col_local = jnp.sum(col_match * ((update_index + LEAD) // grid_cols)[None, :], axis=1)
    col_valid = jnp.sum(col_match, axis=1) > 0
    col_gain = col_valid.astype(jnp.float32)

    lead_tile = current[0, 0]
    slab = tile // grid_rows
    lead_slabs = lead_tile.reshape(grid_rows, slab, tile)
    held = None
    for r in range(grid_rows):
        perm = [
            (i * grid_cols + j, r * grid_cols + LEAD * i + j) for i in range(LEAD) for j in range(LEAD)
        ]
        moved = lax.ppermute(lead_slabs[r], ("row", "col"), perm)
        held = moved if held is None else held + moved
    everything = lax.all_gather(held, ("row", "col"))
    lead_tiles = everything.reshape(grid_rows, LEAD, LEAD, slab, tile)[:, :, :, :, :]
    lead_block = lead_tiles.transpose(1, 0, 3, 2, 4).reshape(lead_w, lead_w)
    chunks = rows_dev * 2
    half = tile // 2
    panel_col = current[:, 0].reshape(chunks, half, tile)
    gathered = lax.all_to_all(panel_col, "col", split_axis=0, concat_axis=0, tiled=True)
    panel_rows = gathered[:LEAD].transpose(1, 0, 2).reshape(half, lead_w)
    my_tile_row = (my_col // 2) * grid_rows + my_row
    live = jnp.where(
        my_tile_row >= LEAD,
        jnp.take(tile_live, jnp.clip(my_tile_row - LEAD, 0, update_count - 1)),
        1,
    ).astype(jnp.float32)
    masked = panel_rows * live
    bound = 1.0 + 10.0 * jnp.sum(masked * masked)
    aug = jnp.concatenate(
        [
            jnp.concatenate([lead_block, jnp.zeros((lead_w, half), jnp.float32)], axis=1),
            jnp.concatenate([masked, jnp.where(jnp.eye(half, dtype=jnp.bool_), bound, 0.0)], axis=1),
        ],
        axis=0,
    )
    aug_factor = lax.linalg.cholesky(aug, symmetrize_input=False)
    chol = aug_factor[:lead_w, :lead_w]
    solved = aug_factor[lead_w:, :lead_w]
    start = jnp.clip(my_tile_row * tile + (my_col % 2) * half, 0, lead_w - half)
    chol_rows = lax.dynamic_slice(chol, (start, 0), (half, lead_w))
    piece = jnp.where(my_tile_row < LEAD, chol_rows, solved)
    copies = jnp.broadcast_to(piece[None], (grid_cols,) + piece.shape)
    factor_rows = lax.all_to_all(copies, "col", split_axis=0, concat_axis=0, tiled=True)
    factor_rows = factor_rows.reshape(rows_dev, tile, lead_w)

    src_row = my_col % grid_rows
    mine = None
    for j in range(grid_rows):
        perm = []
        for c in range(grid_cols):
            s = c % grid_rows
            source_col = 4 * (j // 2) + 2 * (c // grid_rows) + j % 2
            perm.append((s * grid_cols + source_col, ((s + j) % grid_rows) * grid_cols + c))
        moved = lax.ppermute(piece, ("row", "col"), perm)
        mine = moved if mine is None else mine + moved
    ring = [mine]
    for step in range(1, grid_rows // 2):
        perm = [(i, (i + 2 * step) % grid_rows) for i in range(grid_rows)]
        ring.append(lax.ppermute(mine, "row", perm))
    ring = jnp.stack(ring)
    partner = lax.ppermute(ring, "row", [(i, i ^ 1) for i in range(grid_rows)])
    combined = jnp.concatenate([ring, partner], axis=0)
    chunk_ids = jnp.arange(grid_rows, dtype=jnp.int32)
    own_d = (my_row - src_row - chunk_ids) % grid_rows
    par_d = ((my_row ^ 1) - src_row - chunk_ids) % grid_rows
    pos = jnp.where(own_d % 2 == 0, own_d // 2, grid_rows // 2 + par_d // 2)
    col_factor = combined[pos].reshape(cols_dev, tile, lead_w)

    prod = lax.dot_general(
        factor_rows.reshape(rows_dev * tile, lead_w),
        col_factor.reshape(cols_dev * tile, lead_w),
        (((1,), (1,)), ((), ())),
        precision=SCHUR_PRECISION,
    )
    prod = prod.reshape(rows_dev, tile, cols_dev, tile).transpose(0, 2, 1, 3)
    schur = (current - prod).reshape((rows_dev * cols_dev,) + current.shape[2:])

    flat_idx = send_local[:, None] * cols_dev + col_local[None, :]
    outgoing = schur[flat_idx]
    incoming = lax.all_to_all(outgoing, "row", split_axis=0, concat_axis=0, tiled=True)
    keep = (recv_valid[:, None] & col_valid[None, :])[:, :, None, None]
    parent = jnp.stack(
        [
            jnp.where(keep[slot], lax.dynamic_index_in_dim(incoming, recv_source[slot], keepdims=False), 0.0)
            for slot in range(rows_dev)
        ]
    )
    return (factor_rows[:, None], parent[:, None, :, None])


def solution(mesh):
    in_specs = (P(None, "row", None, "col", None, None), P(), P(), P())
    out_specs = (P(None, "row", None, None), P(None, "row", None, "col", None, None))
    return jax.shard_map(local, mesh=mesh, in_specs=in_specs, out_specs=out_specs, check_vma=False)
```

```python
import jax
import jax.numpy as jnp
from jax import lax
from jax.sharding import PartitionSpec as P

LEAD = 4
SCHUR_PRECISION = lax.Precision.HIGH


def valid_gain(valid_flags, ndims):
    return valid_flags.astype(jnp.float32).reshape((-1,) + (1,) * (ndims - 1))


def route_rows(block_now, send_local, send_valid, recv_source, recv_valid, grid_rows):
    outgoing = jnp.take(block_now, send_local, axis=0) * valid_gain(send_valid, block_now.ndim)
    outgoing = outgoing.reshape((grid_rows, -1) + block_now.shape[1:])
    incoming = lax.all_to_all(outgoing, "row", split_axis=0, concat_axis=0, tiled=True)
    incoming = incoming.reshape((-1,) + block_now.shape[1:])
    return jnp.take(incoming, recv_source, axis=0) * valid_gain(recv_valid, block_now.ndim)


def local(front, tile_live, row_target, col_target):
    grid_rows = lax.axis_size("row")
    grid_cols = lax.axis_size("col")
    my_row = lax.axis_index("row")
    my_col = lax.axis_index("col")
    rows_dev = front.shape[0]
    cols_dev = front.shape[2]
    tile = front.shape[4]
    lead_w = LEAD * tile
    per_dest = rows_dev // grid_rows
    current = front[:, 0, :, 0]
    update_count = tile_live.shape[0]

    update_index = jnp.arange(update_count, dtype=jnp.int32)
    source_row = (update_index + LEAD) % grid_rows
    target_row = row_target % grid_rows
    target_slot = row_target // grid_rows
    earlier = (
        (source_row[:, None] == source_row[None, :])
        & (target_row[:, None] == target_row[None, :])
        & (update_index[None, :] < update_index[:, None])
    )
    arrival = jnp.sum(earlier.astype(jnp.int32), axis=1)
    send_slots = jnp.arange(grid_rows * per_dest, dtype=jnp.int32)
    send_match = (
        (source_row[None, :] == my_row)
        & (target_row[None, :] == send_slots[:, None] // per_dest)
        & (arrival[None, :] == send_slots[:, None] % per_dest)
    ).astype(jnp.int32)
    send_local = jnp.sum(send_match * ((update_index + LEAD) // grid_rows)[None, :], axis=1)
    send_valid = jnp.sum(send_match, axis=1) > 0
    out_slots = jnp.arange(rows_dev, dtype=jnp.int32)
    recv_match = (
        (target_row[None, :] == my_row) & (target_slot[None, :] == out_slots[:, None])
    ).astype(jnp.int32)
    recv_source = jnp.sum(recv_match * (source_row * per_dest + arrival)[None, :], axis=1)
    recv_valid = jnp.sum(recv_match, axis=1) > 0
    source_col = (update_index + LEAD) % grid_cols
    out_cols = jnp.arange(cols_dev, dtype=jnp.int32)
    col_match = (
        (source_col[None, :] == my_col) & ((col_target // grid_cols)[None, :] == out_cols[:, None])
    ).astype(jnp.int32)
    col_local = jnp.sum(col_match * ((update_index + LEAD) // grid_cols)[None, :], axis=1)
    col_valid = jnp.sum(col_match, axis=1) > 0
    col_gain = col_valid.astype(jnp.float32)

    lead_tile = current[0, 0]
    slab = tile // grid_rows
    lead_slabs = lead_tile.reshape(grid_rows, slab, tile)
    held = None
    for r in range(grid_rows):
        perm = [
            (i * grid_cols + j, r * grid_cols + LEAD * i + j) for i in range(LEAD) for j in range(LEAD)
        ]
        moved = lax.ppermute(lead_slabs[r], ("row", "col"), perm)
        held = moved if held is None else held + moved
    everything = lax.all_gather(held, ("row", "col"))
    lead_tiles = everything.reshape(grid_rows, LEAD, LEAD, slab, tile)[:, :, :, :, :]
    lead_block = lead_tiles.transpose(1, 0, 3, 2, 4).reshape(lead_w, lead_w)
    chunks = rows_dev * 2
    half = tile // 2
    panel_col = current[:, 0].reshape(chunks, half, tile)
    gathered = lax.all_to_all(panel_col, "col", split_axis=0, concat_axis=0, tiled=True)
    panel_rows = gathered[:LEAD].transpose(1, 0, 2).reshape(half, lead_w)
    my_tile_row = (my_col // 2) * grid_rows + my_row
    live = jnp.where(
        my_tile_row >= LEAD,
        jnp.take(tile_live, jnp.clip(my_tile_row - LEAD, 0, update_count - 1)),
        1,
    ).astype(jnp.float32)
    masked = panel_rows * live
    bound = 1.0 + 10.0 * jnp.sum(masked * masked)
    aug = jnp.concatenate(
        [
            jnp.concatenate([lead_block, jnp.zeros((lead_w, half), jnp.float32)], axis=1),
            jnp.concatenate([masked, jnp.where(jnp.eye(half, dtype=jnp.bool_), bound, 0.0)], axis=1),
        ],
        axis=0,
    )
    aug_factor = lax.linalg.cholesky(aug, symmetrize_input=False)
    chol = aug_factor[:lead_w, :lead_w]
    solved = aug_factor[lead_w:, :lead_w]
    start = jnp.clip(my_tile_row * tile + (my_col % 2) * half, 0, lead_w - half)
    chol_rows = lax.dynamic_slice(chol, (start, 0), (half, lead_w))
    piece = jnp.where(my_tile_row < LEAD, chol_rows, solved)
    factor_rows = lax.all_gather(piece, "col").reshape(rows_dev, tile, lead_w)

    src_row = my_col % grid_rows
    mine = None
    for j in range(grid_rows):
        perm = []
        for c in range(grid_cols):
            s = c % grid_rows
            source_col = 4 * (j // 2) + 2 * (c // grid_rows) + j % 2
            perm.append((s * grid_cols + source_col, ((s + j) % grid_rows) * grid_cols + c))
        moved = lax.ppermute(piece, ("row", "col"), perm)
        mine = moved if mine is None else mine + moved
    ring = [mine]
    for step in range(1, grid_rows // 2):
        perm = [(i, (i + 2 * step) % grid_rows) for i in range(grid_rows)]
        ring.append(lax.ppermute(mine, "row", perm))
    ring = jnp.stack(ring)
    partner = lax.ppermute(ring, "row", [(i, i ^ 1) for i in range(grid_rows)])
    combined = jnp.concatenate([ring, partner], axis=0)
    chunk_ids = jnp.arange(grid_rows, dtype=jnp.int32)
    own_d = (my_row - src_row - chunk_ids) % grid_rows
    par_d = ((my_row ^ 1) - src_row - chunk_ids) % grid_rows
    pos = jnp.where(own_d % 2 == 0, own_d // 2, grid_rows // 2 + par_d // 2)
    col_factor = combined[pos].reshape(cols_dev, tile, lead_w)

    prod = lax.dot_general(
        factor_rows.reshape(rows_dev * tile, lead_w),
        col_factor.reshape(cols_dev * tile, lead_w),
        (((1,), (1,)), ((), ())),
        precision=SCHUR_PRECISION,
    )
    prod = prod.reshape(rows_dev, tile, cols_dev, tile).transpose(0, 2, 1, 3)
    schur = (current - prod).reshape((rows_dev * cols_dev,) + current.shape[2:])

    flat_idx = send_local[:, None] * cols_dev + col_local[None, :]
    outgoing = jnp.stack(
        [
            jnp.stack(
                [lax.dynamic_index_in_dim(schur, flat_idx[slot, b], keepdims=False) for b in range(cols_dev)]
            )
            for slot in range(rows_dev)
        ]
    )
    incoming = lax.all_to_all(outgoing, "row", split_axis=0, concat_axis=0, tiled=True)
    keep = (recv_valid[:, None] & col_valid[None, :])[:, :, None, None]
    parent = jnp.stack(
        [
            jnp.where(keep[slot], lax.dynamic_index_in_dim(incoming, recv_source[slot], keepdims=False), 0.0)
            for slot in range(rows_dev)
        ]
    )
    return (factor_rows[:, None], parent[:, None, :, None])


def solution(mesh):
    in_specs = (P(None, "row", None, "col", None, None), P(), P(), P())
    out_specs = (P(None, "row", None, None), P(None, "row", None, "col", None, None))
    return jax.shard_map(local, mesh=mesh, in_specs=in_specs, out_specs=out_specs, check_vma=False)
```
